256 devices in a mesh: tm: 8 (over y, core), node: 32 (over z, x).
Axes of the slice: x: 4, y: 4, z: 8, core: 2. Of those that a mesh axis runs over, the one named last changes fastest.
Arguments:
- inputs: bfloat16 [32768, 2048], P('node', 'tm'), may hold values from -6 to 6
- conv_weight: bfloat16 [3, 64, 256], replicated, may hold values from -0.4375 to 0.4375
- conv_bias: float32 [256], replicated, may hold values from -3 to 3
- tile_values: bfloat16 [256, 4, 128, 128], P('node'), may hold values from -0.25 to 0.25
- tile_cols: int32 [256, 4], P('node'), may hold values from -2 to 257, as said below
- tile_count: int32 [256], P('node'), may hold values from 1 to 4, as said below
- cheb_weight: bfloat16 [3, 128, 128], replicated, may hold values from -0.3125 to 0.3125
- cheb_bias: float32 [128], replicated, may hold values from -3 to 3
Outputs:
- graph_out: bfloat16 [32768, 32, 128], P('node', 'tm')
The draws below stay inside these ranges and needn't reach their ends.
Inputs may be any that keep to these rules, and one draw needn't show every extreme that they name: `tile_cols`: tile 0 of block b names b itself; tiles 1 to 3 name b plus distinct nonzero offsets in -2 to 2. Tile slots at or after tile_count[b] are unused.
All inputs are finite; a program needn't handle non-finite values.
Results may differ from the reference program's by a relative error of at most 0.0056.
Values may be sent and summed in bfloat16 or wider, within the bound.
No kernel may reach another device: no remote copies, remote signals or barrier semaphores. Data moves between devices by JAX's collectives and lax.ppermute only.
A program may use at most 64 MiB of HBM per device.

```python
import jax
import jax.numpy as jnp
from jax import lax

C_IN = 64
C_OUT = 128
BLOCK = 128
HB = 2
TPB = 4
NB_DEV = 8
NBLK = 256
NODES = 32768
TIME = 32


def draw_tile_cols(key, part):
    offsets = jnp.concatenate([jnp.arange(-HB, 0), jnp.arange(1, HB + 1)]).astype(jnp.int32)
    scores = jax.random.randint(key, (NBLK, 2 * HB), 0, 1 << 20)
    row_index = jnp.arange(NBLK, dtype=jnp.int32)[:, None]
    col_index = jnp.arange(2 * HB, dtype=jnp.int32)[None, :]
    forced = (row_index == 0) & (col_index == 0) | (row_index == NBLK - 1) & (col_index == 2 * HB - 1)
    scores = jnp.where(forced, -1, scores)
    scores = scores * (2 * HB) + col_index
    ranking = jnp.argsort(scores, axis=1)
    picked = offsets[ranking[:, :TPB - 1]]
    row_ids = jnp.arange(NBLK, dtype=jnp.int32)[:, None]
    return jnp.concatenate([row_ids, row_ids + picked], axis=1).astype(jnp.int32)


def draw_tile_count(key, part):
    drawn = jax.random.randint(key, (NBLK,), 1, TPB + 1)
    group_id = jnp.arange(NBLK) // NB_DEV
    full_rows = group_id % 4 == 0
    return jnp.where(full_rows, TPB, drawn).astype(jnp.int32)


def levels(own_key, shape, pieces, smallest, top_value):
    factor_of = 1.0
    for axis_at, parts in pieces:
        heights = jax.random.uniform(jax.random.fold_in(jax.random.fold_in(own_key, 6), axis_at), (parts,), jnp.float32, smallest / len(pieces), top_value / len(pieces))
        factor_of = factor_of * jnp.repeat(jnp.exp(heights), shape[axis_at] // parts).reshape((-1,) + (1,) * (len(shape) - 1 - axis_at))
    return factor_of


def centred(key, shape, scale, limit, cuts=(), kind=jnp.bfloat16):
    values = jax.random.normal(key, shape, jnp.float32) * scale
    if len(cuts) > 0:
        values = levels(key, shape, cuts, -0.22, 0.18) * values
    return jnp.clip(values, min=-limit, max=limit).astype(kind)


def setup_inputs(seed: int = 0) -> dict:
    splits = jax.random.split(jax.random.key(seed), 9)
    inputs = centred(splits[0], (NODES, TIME * C_IN), 1.0, 6.0, ((0, 32), (1, 8)))
    conv_weight = centred(splits[1], (3, C_IN, 2 * C_OUT), (3 * C_IN) ** -0.5, 0.4375)
    conv_bias = centred(splits[2], (2 * C_OUT,), 0.5, 3.0, (), jnp.float32)
    tile_values = centred(splits[3], (NBLK, TPB, BLOCK, BLOCK), (BLOCK * TPB) ** -0.5, 0.25, ((0, 32),))
    tile_cols = draw_tile_cols(jax.random.fold_in(splits[8], 71), 0)
    tile_count = draw_tile_count(jax.random.fold_in(splits[8], 71), 0)
    cheb_weight = centred(splits[6], (3, C_OUT, C_OUT), (3 * C_OUT) ** -0.5, 0.3125)
    cheb_bias = centred(splits[7], (C_OUT,), 0.5, 3.0, (), jnp.float32)
    return {"inputs": inputs, "conv_weight": conv_weight, "conv_bias": conv_bias, "tile_values": tile_values, "tile_cols": tile_cols, "tile_count": tile_count, "cheb_weight": cheb_weight, "cheb_bias": cheb_bias}


def conv_block(x_block, conv_weight, conv_bias):
    by_time = x_block.reshape(BLOCK, TIME, C_IN)
    widened = jnp.pad(by_time, ((0, 0), (4, 0), (0, 0)))
    stacked = jnp.concatenate([widened[:, 4:], widened[:, 2:2 + TIME], widened[:, :TIME]], axis=-1)
    stacked = stacked.reshape(BLOCK * TIME, 3 * C_IN)
    mixed_out = jnp.dot(stacked, conv_weight.reshape(3 * C_IN, 2 * C_OUT), preferred_element_type=jnp.float32) + conv_bias
    mixed_out = mixed_out.reshape(BLOCK, TIME, 2 * C_OUT)
    carried = jnp.pad(by_time.astype(jnp.float32), ((0, 0), (0, 0), (0, C_OUT - C_IN)))
    linear = mixed_out[..., :C_OUT] + carried
    gated = linear * jax.nn.sigmoid(mixed_out[..., C_OUT:])
    return gated.astype(jnp.bfloat16).reshape(BLOCK, TIME * C_OUT)


def propagate(features, tile_values, tile_cols, tile_count):
    padded = jnp.pad(features, ((HB, HB), (0, 0), (0, 0)))

    def per_block(bundle):
        tile_set, col_ids, live_count = bundle
        total = jnp.zeros((BLOCK, TIME * C_OUT), jnp.float32)
        for tile_slot in range(TPB):
            start = (col_ids[tile_slot] + HB).astype(jnp.int32)
            column_block = lax.dynamic_slice_in_dim(padded, start, 1, 0)[0]
            live_flag = (tile_slot < live_count).astype(jnp.float32)
            total = total + live_flag * jnp.dot(tile_set[tile_slot], column_block, preferred_element_type=jnp.float32)
        return total

    return lax.map(per_block, (tile_values, tile_cols, tile_count))


def reference(inputs, conv_weight, conv_bias, tile_values, tile_cols, tile_count, cheb_weight, cheb_bias):
    features = lax.map(lambda x_block: conv_block(x_block, conv_weight, conv_bias), inputs.reshape(NBLK, BLOCK, TIME * C_IN))
    order_one = propagate(features, tile_values, tile_cols, tile_count).astype(jnp.bfloat16)
    order_two = propagate(order_one, tile_values, tile_cols, tile_count)
    cheb_two = (2.0 * order_two - features.astype(jnp.float32)).astype(jnp.bfloat16)
    flat_weight = cheb_weight.reshape(3 * C_OUT, C_OUT)

    def finish(bundle):
        zero_part, one_part, two_part = bundle
        joined = jnp.concatenate([zero_part.reshape(BLOCK * TIME, C_OUT), one_part.reshape(BLOCK * TIME, C_OUT), two_part.reshape(BLOCK * TIME, C_OUT)], axis=-1)
        result = jnp.dot(joined, flat_weight, preferred_element_type=jnp.float32) + cheb_bias
        return jax.nn.relu(result).astype(jnp.bfloat16).reshape(BLOCK, TIME, C_OUT)

    graph_out = lax.map(finish, (features, order_one, cheb_two))
    return graph_out.reshape(NODES, TIME, C_OUT)
```

```python
import jax
import jax.numpy as jnp
from jax import lax
from jax.sharding import PartitionSpec as P

HB = 2
TPB = 4


def with_halo(cells, sides, width):
    for axis, dim in sides:
        count = lax.axis_size(axis)
        ends = count - 1
        head = lax.slice_in_dim(cells, 0, width, axis=dim)
        tail = lax.slice_in_dim(cells, cells.shape[dim] - width, cells.shape[dim], axis=dim)
        cells = jnp.concatenate(
            [
                lax.ppermute(tail, axis, [(i, (i + 1) % count) for i in range(ends)]),
                cells,
                lax.ppermute(head, axis, [((i + 1) % count, i) for i in range(ends)]),
            ],
            axis=dim,
        )
    return cells


def passed_along(value, axis, by):
    length = lax.axis_size(axis)
    pairs = [(i, i + by) for i in range(length) if 0 <= i + by < length]
    return lax.ppermute(value, axis, pairs)


def build_band(tile_set, col_ids, live_count, first_block):
    block_count = tile_set.shape[0]
    row_ids = first_block + jnp.arange(block_count, dtype=jnp.int32)
    offset = col_ids - row_ids[:, None] + HB
    live_mask = jnp.arange(TPB, dtype=jnp.int32)[None, :] < live_count[:, None]
    one_hot = (
        offset[:, :, None] == jnp.arange(2 * HB + 1, dtype=jnp.int32)[None, None, :]
    ) & live_mask[:, :, None]
    band_tiles = jnp.einsum(
        "bjo,bjpq->bopq", one_hot.astype(jnp.bfloat16), tile_set, preferred_element_type=jnp.float32
    )
    return band_tiles.astype(jnp.bfloat16)


def band_product(band_tiles, extended):
    block_count = band_tiles.shape[0]
    total = jnp.einsum(
        "bpq,bqf->bpf",
        band_tiles[:, 0],
        extended[0:block_count],
        preferred_element_type=jnp.float32,
    )
    for offset in range(1, 2 * HB + 1):
        total = total + jnp.einsum(
            "bpq,bqf->bpf",
            band_tiles[:, offset],
            extended[offset : offset + block_count],
            preferred_element_type=jnp.float32,
        )
    return total


def fetch_rim(values, block_rows):
    return with_halo(values, (("node", 0),), HB * block_rows)


def pair_weight(conv_weight):
    taps, chan_in, width = conv_weight.shape
    eye = jnp.eye(2, dtype=conv_weight.dtype)
    blocks = [jnp.kron(eye, conv_weight[k]) for k in range(taps)]
    rows_in = jnp.arange(2 * chan_in, dtype=jnp.int32)[:, None]
    cols_out = jnp.arange(2 * width, dtype=jnp.int32)[None, :]
    place = (cols_out == rows_in // chan_in * width + rows_in % chan_in).astype(conv_weight.dtype)
    return jnp.concatenate(blocks + [place], axis=0)


def block_diag(weight, steps):
    return jnp.kron(jnp.eye(steps, dtype=weight.dtype), weight)


def shards(
    inputs, conv_weight, conv_bias, tile_values, tile_cols, tile_count, cheb_weight, cheb_bias
):
    row_count, flat_width = inputs.shape
    chan_in = conv_weight.shape[1]
    chan_out = cheb_weight.shape[2]
    steps_dev = flat_width // chan_in
    block_count, block_rows = (tile_values.shape[0], tile_values.shape[2])
    feat_width = steps_dev * chan_out
    earlier = passed_along(inputs, "tm", 1)
    window = jnp.concatenate([earlier, inputs], axis=1)
    wpair = pair_weight(conv_weight)
    pair_w = 2 * chan_in
    pieces = []
    for p in range(steps_dev // 2):
        base = steps_dev * chan_in + p * pair_w
        newest = window[:, base : base + pair_w]
        middle = window[:, base - pair_w : base]
        oldest = window[:, base - 2 * pair_w : base - pair_w]
        lhs = jnp.concatenate([newest, middle, oldest, newest], axis=1)
        mixed = jnp.dot(lhs, wpair, preferred_element_type=jnp.float32)
        for tt in range(2):
            lo = tt * 2 * chan_out
            linear = mixed[:, lo : lo + chan_out] + conv_bias[:chan_out]
            gate = mixed[:, lo + chan_out : lo + 2 * chan_out] + conv_bias[chan_out:]
            pieces.append(linear * jax.nn.sigmoid(gate))
    flat_features = jnp.concatenate(pieces, axis=1).astype(jnp.bfloat16)
    first_block = lax.axis_index("node") * block_count

    band_tiles = build_band(tile_values, tile_cols, tile_count, first_block)
    extended = fetch_rim(flat_features, block_rows).reshape(
        block_count + 2 * HB, block_rows, feat_width
    )
    order_one = band_product(band_tiles, extended).astype(jnp.bfloat16)
    one_ext = fetch_rim(order_one.reshape(row_count, feat_width), block_rows).reshape(
        block_count + 2 * HB, block_rows, feat_width
    )
    order_two = band_product(band_tiles, one_ext)
    by_block = flat_features.reshape(block_count, block_rows, feat_width)
    cheb_two = (2.0 * order_two - by_block.astype(jnp.float32)).astype(jnp.bfloat16)
    joined = jnp.concatenate(
        [flat_features, order_one.reshape(row_count, feat_width), cheb_two.reshape(row_count, feat_width)],
        axis=1,
    )
    wfinal = jnp.concatenate([block_diag(cheb_weight[k], steps_dev) for k in range(3)], axis=0)
    result = jnp.dot(joined, wfinal, preferred_element_type=jnp.float32)
    result = result + jnp.tile(cheb_bias, steps_dev)
    return jax.nn.relu(result).astype(jnp.bfloat16).reshape(row_count, steps_dev, chan_out)


def solution(mesh):
    placed = (
        P("node", "tm"),
        P(),
        P(),
        P("node", None, None, None),
        P("node", None),
        P("node"),
        P(),
        P(),
    )
    return jax.shard_map(
        shards, mesh=mesh, in_specs=placed, out_specs=P("node", "tm", None), check_vma=False
    )
```

```python
import jax
import jax.numpy as jnp
from jax import lax
from jax.sharding import PartitionSpec as P

HB = 2
TPB = 4


def with_halo(cells, sides, width):
    for axis, dim in sides:
        count = lax.axis_size(axis)
        ends = count - 1
        head = lax.slice_in_dim(cells, 0, width, axis=dim)
        tail = lax.slice_in_dim(cells, cells.shape[dim] - width, cells.shape[dim], axis=dim)
        cells = jnp.concatenate(
            [
                lax.ppermute(tail, axis, [(i, (i + 1) % count) for i in range(ends)]),
                cells,
                lax.ppermute(head, axis, [((i + 1) % count, i) for i in range(ends)]),
            ],
            axis=dim,
        )
    return cells


def passed_along(value, axis, by):
    length = lax.axis_size(axis)
    pairs = [(i, i + by) for i in range(length) if 0 <= i + by < length]
    return lax.ppermute(value, axis, pairs)


def build_band(tile_set, col_ids, live_count, first_block):
    block_count = tile_set.shape[0]
    row_ids = first_block + jnp.arange(block_count, dtype=jnp.int32)
    offset = col_ids - row_ids[:, None] + HB
    live_mask = jnp.arange(TPB, dtype=jnp.int32)[None, :] < live_count[:, None]
    one_hot = (
        offset[:, :, None] == jnp.arange(2 * HB + 1, dtype=jnp.int32)[None, None, :]
    ) & live_mask[:, :, None]
    band_tiles = jnp.einsum(
        "bjo,bjpq->bopq", one_hot.astype(jnp.bfloat16), tile_set, preferred_element_type=jnp.float32
    )
    return band_tiles.astype(jnp.bfloat16)


def band_product(band_tiles, extended):
    block_count = band_tiles.shape[0]
    total = jnp.einsum(
        "bpq,bqf->bpf",
        band_tiles[:, 0],
        extended[0:block_count],
        preferred_element_type=jnp.float32,
    )
    for offset in range(1, 2 * HB + 1):
        total = total + jnp.einsum(
            "bpq,bqf->bpf",
            band_tiles[:, offset],
            extended[offset : offset + block_count],
            preferred_element_type=jnp.float32,
        )
    return total


def fetch_rim(values, block_rows):
    return with_halo(values, (("node", 0),), HB * block_rows)


def pair_weight(conv_weight):
    taps, chan_in, width = conv_weight.shape
    eye = jnp.eye(2, dtype=conv_weight.dtype)
    blocks = [jnp.kron(eye, conv_weight[k]) for k in range(taps)]
    rows_in = jnp.arange(2 * chan_in, dtype=jnp.int32)[:, None]
    cols_out = jnp.arange(2 * width, dtype=jnp.int32)[None, :]
    place = (cols_out == rows_in // chan_in * width + rows_in % chan_in).astype(conv_weight.dtype)
    return jnp.concatenate(blocks + [place], axis=0)


def block_diag(weight, steps):
    return jnp.kron(jnp.eye(steps, dtype=weight.dtype), weight)


def shards(
    inputs, conv_weight, conv_bias, tile_values, tile_cols, tile_count, cheb_weight, cheb_bias
):
    row_count, flat_width = inputs.shape
    chan_in = conv_weight.shape[1]
    chan_out = cheb_weight.shape[2]
    steps_dev = flat_width // chan_in
    block_count, block_rows = (tile_values.shape[0], tile_values.shape[2])
    feat_width = steps_dev * chan_out
    node = lax.axis_index("node")
    node_count = lax.axis_size("node")
    tm_count = lax.axis_size("tm")
    first_block = node * block_count
    rim = HB * block_rows
    head = inputs[:rim]
    tail = inputs[row_count - rim :]
    to_right = [(i, i + 1) for i in range(node_count - 1)]
    to_left = [(i + 1, i) for i in range(node_count - 1)]
    diag_right = [
        (j * node_count + i, (j + 1) * node_count + i + 1)
        for i in range(node_count - 1)
        for j in range(tm_count - 1)
    ]
    diag_left = [
        (j * node_count + i + 1, (j + 1) * node_count + i)
        for i in range(node_count - 1)
        for j in range(tm_count - 1)
    ]
    cur_left = lax.ppermute(tail, "node", to_right)
    cur_right = lax.ppermute(head, "node", to_left)
    prev_own = passed_along(inputs, "tm", 1)
    prev_left = lax.ppermute(tail, ("tm", "node"), diag_right)
    prev_right = lax.ppermute(head, ("tm", "node"), diag_left)
    cur_ext = jnp.concatenate([cur_left, inputs, cur_right], axis=0)
    prev_ext = jnp.concatenate([prev_left, prev_own, prev_right], axis=0)
    window = jnp.concatenate([prev_ext, cur_ext], axis=1)
    wpair = pair_weight(conv_weight)
    pair_w = 2 * chan_in
    pieces = []
    for p in range(steps_dev // 2):
        base = steps_dev * chan_in + p * pair_w
        newest = window[:, base : base + pair_w]
        middle = window[:, base - pair_w : base]
        oldest = window[:, base - 2 * pair_w : base - pair_w]
        lhs = jnp.concatenate([newest, middle, oldest, newest], axis=1)
        mixed = jnp.dot(lhs, wpair, preferred_element_type=jnp.float32)
        for tt in range(2):
            lo = tt * 2 * chan_out
            linear = mixed[:, lo : lo + chan_out] + conv_bias[:chan_out]
            gate = mixed[:, lo + chan_out : lo + 2 * chan_out] + conv_bias[chan_out:]
            pieces.append(linear * jax.nn.sigmoid(gate))
    ext_rows = row_count + 2 * rim
    ext_block = first_block - HB + jnp.arange(ext_rows, dtype=jnp.int32) // block_rows
    inside = (ext_block >= 0) & (ext_block < node_count * block_count)
    feat_ext = jnp.where(inside[:, None], jnp.concatenate(pieces, axis=1), 0.0).astype(jnp.bfloat16)
    flat_features = feat_ext[rim : rim + row_count]

    band_tiles = build_band(tile_values, tile_cols, tile_count, first_block)
    extended = feat_ext.reshape(block_count + 2 * HB, block_rows, feat_width)
    order_one = band_product(band_tiles, extended).astype(jnp.bfloat16)
    one_ext = fetch_rim(order_one.reshape(row_count, feat_width), block_rows).reshape(
        block_count + 2 * HB, block_rows, feat_width
    )
    order_two = band_product(band_tiles, one_ext)
    by_block = flat_features.reshape(block_count, block_rows, feat_width)
    cheb_two = (2.0 * order_two - by_block.astype(jnp.float32)).astype(jnp.bfloat16)
    joined = jnp.concatenate(
        [flat_features, order_one.reshape(row_count, feat_width), cheb_two.reshape(row_count, feat_width)],
        axis=1,
    )
    wfinal = jnp.concatenate([block_diag(cheb_weight[k], steps_dev) for k in range(3)], axis=0)
    result = jnp.dot(joined, wfinal, preferred_element_type=jnp.float32)
    result = result + jnp.tile(cheb_bias, steps_dev)
    return jax.nn.relu(result).astype(jnp.bfloat16).reshape(row_count, steps_dev, chan_out)


def solution(mesh):
    placed = (
        P("node", "tm"),
        P(),
        P(),
        P("node", None, None, None),
        P("node", None),
        P("node"),
        P(),
        P(),
    )
    return jax.shard_map(
        shards, mesh=mesh, in_specs=placed, out_specs=P("node", "tm", None), check_vma=False
    )
```

```python
import jax
import jax.numpy as jnp
from jax import lax
from jax.sharding import PartitionSpec as P

HB = 2
TPB = 4


def with_halo(cells, sides, width):
    for axis, dim in sides:
        count = lax.axis_size(axis)
        ends = count - 1
        head = lax.slice_in_dim(cells, 0, width, axis=dim)
        tail = lax.slice_in_dim(cells, cells.shape[dim] - width, cells.shape[dim], axis=dim)
        cells = jnp.concatenate(
            [
                lax.ppermute(tail, axis, [(i, (i + 1) % count) for i in range(ends)]),
                cells,
                lax.ppermute(head, axis, [((i + 1) % count, i) for i in range(ends)]),
            ],
            axis=dim,
        )
    return cells


def passed_along(value, axis, by):
    length = lax.axis_size(axis)
    pairs = [(i, i + by) for i in range(length) if 0 <= i + by < length]
    return lax.ppermute(value, axis, pairs)


def build_band(tile_set, col_ids, live_count, first_block):
    block_count = tile_set.shape[0]
    row_ids = first_block + jnp.arange(block_count, dtype=jnp.int32)
    offset = col_ids - row_ids[:, None] + HB
    live_mask = jnp.arange(TPB, dtype=jnp.int32)[None, :] < live_count[:, None]
    one_hot = (
        offset[:, :, None] == jnp.arange(2 * HB + 1, dtype=jnp.int32)[None, None, :]
    ) & live_mask[:, :, None]
    band_tiles = jnp.einsum(
        "bjo,bjpq->bopq", one_hot.astype(jnp.bfloat16), tile_set, preferred_element_type=jnp.float32
    )
    return band_tiles.astype(jnp.bfloat16)


def band_product(band_tiles, extended):
    block_count = band_tiles.shape[0]
    total = jnp.einsum(
        "bpq,bqf->bpf",
        band_tiles[:, 0],
        extended[0:block_count],
        preferred_element_type=jnp.float32,
    )
    for offset in range(1, 2 * HB + 1):
        total = total + jnp.einsum(
            "bpq,bqf->bpf",
            band_tiles[:, offset],
            extended[offset : offset + block_count],
            preferred_element_type=jnp.float32,
        )
    return total


def fetch_rim(values, block_rows):
    return with_halo(values, (("node", 0),), HB * block_rows)


def pair_weight(conv_weight):
    taps, chan_in, width = conv_weight.shape
    eye = jnp.eye(2, dtype=conv_weight.dtype)
    blocks = [jnp.kron(eye, conv_weight[k]) for k in range(taps)]
    rows_in = jnp.arange(2 * chan_in, dtype=jnp.int32)[:, None]
    cols_out = jnp.arange(2 * width, dtype=jnp.int32)[None, :]
    place = (cols_out == rows_in // chan_in * width + rows_in % chan_in).astype(conv_weight.dtype)
    return jnp.concatenate(blocks + [place], axis=0)


def block_diag(weight, steps):
    return jnp.kron(jnp.eye(steps, dtype=weight.dtype), weight)


def shards(
    inputs, conv_weight, conv_bias, tile_values, tile_cols, tile_count, cheb_weight, cheb_bias
):
    row_count, flat_width = inputs.shape
    chan_in = conv_weight.shape[1]
    chan_out = cheb_weight.shape[2]
    steps_dev = flat_width // chan_in
    block_count, block_rows = (tile_values.shape[0], tile_values.shape[2])
    feat_width = steps_dev * chan_out
    earlier = passed_along(inputs, "tm", 1)
    window = jnp.concatenate([earlier, inputs], axis=1)
    wpair = pair_weight(conv_weight)
    pair_w = 2 * chan_in
    pieces = []
    for p in range(steps_dev // 2):
        base = steps_dev * chan_in + p * pair_w
        newest = window[:, base : base + pair_w]
        middle = window[:, base - pair_w : base]
        oldest = window[:, base - 2 * pair_w : base - pair_w]
        lhs = jnp.concatenate([newest, middle, oldest, newest], axis=1)
        mixed = jnp.dot(lhs, wpair, preferred_element_type=jnp.float32)
        for tt in range(2):
            lo = tt * 2 * chan_out
            linear = mixed[:, lo : lo + chan_out] + conv_bias[:chan_out]
            gate = mixed[:, lo + chan_out : lo + 2 * chan_out] + conv_bias[chan_out:]
            pieces.append(linear * jax.nn.sigmoid(gate))
    flat_features = jnp.concatenate(pieces, axis=1).astype(jnp.bfloat16)
    first_block = lax.axis_index("node") * block_count

    band_tiles = build_band(tile_values, tile_cols, tile_count, first_block)
    node_count = lax.axis_size("node")
    to_right = [(i, i + 1) for i in range(node_count - 1)]
    to_left = [(i + 1, i) for i in range(node_count - 1)]
    band_left = lax.ppermute(band_tiles[block_count - HB :], "node", to_right)
    band_right = lax.ppermute(band_tiles[:HB], "node", to_left)
    reach = 2 * HB * block_rows
    feat_left = lax.ppermute(flat_features[row_count - reach :], "node", to_right)
    feat_right = lax.ppermute(flat_features[:reach], "node", to_left)
    feat_ext = jnp.concatenate([feat_left, flat_features, feat_right], axis=0).reshape(
        block_count + 4 * HB, block_rows, feat_width
    )
    band_ext = jnp.concatenate([band_left, band_tiles, band_right], axis=0)
    one_ext = band_product(band_ext, feat_ext).astype(jnp.bfloat16)
    order_two = band_product(band_tiles, one_ext)
    order_one = one_ext[HB : HB + block_count]
    by_block = flat_features.reshape(block_count, block_rows, feat_width)
    cheb_two = (2.0 * order_two - by_block.astype(jnp.float32)).astype(jnp.bfloat16)
    joined = jnp.concatenate(
        [flat_features, order_one.reshape(row_count, feat_width), cheb_two.reshape(row_count, feat_width)],
        axis=1,
    )
    wfinal = jnp.concatenate([block_diag(cheb_weight[k], steps_dev) for k in range(3)], axis=0)
    result = jnp.dot(joined, wfinal, preferred_element_type=jnp.float32)
    result = result + jnp.tile(cheb_bias, steps_dev)
    return jax.nn.relu(result).astype(jnp.bfloat16).reshape(row_count, steps_dev, chan_out)


def solution(mesh):
    placed = (
        P("node", "tm"),
        P(),
        P(),
        P("node", None, None, None),
        P("node", None),
        P("node"),
        P(),
        P(),
    )
    return jax.shard_map(
        shards, mesh=mesh, in_specs=placed, out_specs=P("node", "tm", None), check_vma=False
    )
```

```python
import jax
import jax.numpy as jnp
from jax import lax
from jax.sharding import PartitionSpec as P
from jax.experimental import pallas as pl
from jax.experimental.pallas import tpu as pltpu

HB = 2
TPB = 4


def with_halo(cells, sides, width):
    for axis, dim in sides:
        count = lax.axis_size(axis)
        ends = count - 1
        head = lax.slice_in_dim(cells, 0, width, axis=dim)
        tail = lax.slice_in_dim(cells, cells.shape[dim] - width, cells.shape[dim], axis=dim)
        cells = jnp.concatenate(
            [
                lax.ppermute(tail, axis, [(i, (i + 1) % count) for i in range(ends)]),
                cells,
                lax.ppermute(head, axis, [((i + 1) % count, i) for i in range(ends)]),
            ],
            axis=dim,
        )
    return cells


def passed_along(value, axis, by):
    length = lax.axis_size(axis)
    pairs = [(i, i + by) for i in range(length) if 0 <= i + by < length]
    return lax.ppermute(value, axis, pairs)


def build_band(tile_set, col_ids, live_count, first_block):
    block_count = tile_set.shape[0]
    row_ids = first_block + jnp.arange(block_count, dtype=jnp.int32)
    offset = col_ids - row_ids[:, None] + HB
    live_mask = jnp.arange(TPB, dtype=jnp.int32)[None, :] < live_count[:, None]
    one_hot = (
        offset[:, :, None] == jnp.arange(2 * HB + 1, dtype=jnp.int32)[None, None, :]
    ) & live_mask[:, :, None]
    band_tiles = jnp.einsum(
        "bjo,bjpq->bopq", one_hot.astype(jnp.bfloat16), tile_set, preferred_element_type=jnp.float32
    )
    return band_tiles.astype(jnp.bfloat16)


def band_product(band_tiles, extended):
    block_count = band_tiles.shape[0]
    total = jnp.einsum(
        "bpq,bqf->bpf",
        band_tiles[:, 0],
        extended[0:block_count],
        preferred_element_type=jnp.float32,
    )
    for offset in range(1, 2 * HB + 1):
        total = total + jnp.einsum(
            "bpq,bqf->bpf",
            band_tiles[:, offset],
            extended[offset : offset + block_count],
            preferred_element_type=jnp.float32,
        )
    return total


def _source(b, o, nb, left_ref, own_ref, right_ref, rows):
    j = b + o - HB
    if j < 0:
        return left_ref, (j + HB) * rows
    if j >= nb:
        return right_ref, (j - nb) * rows
    return own_ref, j * rows


def _band_sum(b, band_ref, left_ref, own_ref, right_ref):
    nb = band_ref.shape[0]
    rows = band_ref.shape[2]
    acc = None
    for o in range(2 * HB + 1):
        src, r0 = _source(b, o, nb, left_ref, own_ref, right_ref, rows)
        term = jnp.dot(band_ref[b, o], src[r0 : r0 + rows, :], preferred_element_type=jnp.float32)
        acc = term if acc is None else acc + term
    return acc


def _first_kernel(band_ref, left_ref, own_ref, right_ref, out_ref):
    nb, rows = band_ref.shape[0], band_ref.shape[2]
    for b in range(nb):
        acc = _band_sum(b, band_ref, left_ref, own_ref, right_ref)
        out_ref[b * rows : (b + 1) * rows, :] = acc.astype(out_ref.dtype)


def _second_kernel(band_ref, left_ref, own_ref, right_ref, feat_ref, weight_ref, bias_ref, out_ref):
    nb, rows = band_ref.shape[0], band_ref.shape[2]
    chan = weight_ref.shape[1]
    steps = own_ref.shape[1] // chan
    bias = bias_ref[...]
    for b in range(nb):
        acc = _band_sum(b, band_ref, left_ref, own_ref, right_ref)
        lo, hi = b * rows, (b + 1) * rows
        feat = feat_ref[lo:hi, :]
        cheb_two = (2.0 * acc - feat.astype(jnp.float32)).astype(jnp.bfloat16)
        one = own_ref[lo:hi, :]
        for t in range(steps):
            cols = slice(t * chan, (t + 1) * chan)
            joined = jnp.concatenate([feat[:, cols], one[:, cols], cheb_two[:, cols]], axis=1)
            res = jnp.dot(joined, weight_ref[...], preferred_element_type=jnp.float32) + bias
            out_ref[lo:hi, cols] = jnp.maximum(res, 0.0).astype(out_ref.dtype)


def _vmem_specs(count):
    return [pl.BlockSpec(memory_space=pltpu.VMEM) for _ in range(count)]


def first_product(band_tiles, left, own, right):
    rows, width = own.shape
    flops = 2 * band_tiles.shape[0] * (2 * HB + 1) * band_tiles.shape[2] ** 2 * width
    return pl.pallas_call(
        _first_kernel,
        out_shape=jax.ShapeDtypeStruct((rows, width), jnp.bfloat16),
        in_specs=_vmem_specs(4),
        out_specs=pl.BlockSpec(memory_space=pltpu.VMEM),
        cost_estimate=pl.CostEstimate(flops=flops, transcendentals=0, bytes_accessed=6 * rows * width),
    )(band_tiles, left, own, right)


def second_product(band_tiles, left, own, right, features, cheb_weight, cheb_bias):
    rows, width = own.shape
    weight = cheb_weight.reshape(-1, cheb_weight.shape[2])
    bias = cheb_bias.reshape(1, -1)
    flops = 2 * band_tiles.shape[0] * (2 * HB + 1) * band_tiles.shape[2] ** 2 * width
    flops += 2 * rows * width * weight.shape[0]
    return pl.pallas_call(
        _second_kernel,
        out_shape=jax.ShapeDtypeStruct((rows, width), jnp.bfloat16),
        in_specs=_vmem_specs(7),
        out_specs=pl.BlockSpec(memory_space=pltpu.VMEM),
        cost_estimate=pl.CostEstimate(flops=flops, transcendentals=0, bytes_accessed=8 * rows * width),
    )(band_tiles, left, own, right, features, weight, bias)


def fetch_rim(values, block_rows):
    return with_halo(values, (("node", 0),), HB * block_rows)


def pair_weight(conv_weight):
    taps, chan_in, width = conv_weight.shape
    eye = jnp.eye(2, dtype=conv_weight.dtype)
    blocks = [jnp.kron(eye, conv_weight[k]) for k in range(taps)]
    rows_in = jnp.arange(2 * chan_in, dtype=jnp.int32)[:, None]
    cols_out = jnp.arange(2 * width, dtype=jnp.int32)[None, :]
    place = (cols_out == rows_in // chan_in * width + rows_in % chan_in).astype(conv_weight.dtype)
    return jnp.concatenate(blocks + [place], axis=0)


def block_diag(weight, steps):
    return jnp.kron(jnp.eye(steps, dtype=weight.dtype), weight)


def shards(
    inputs, conv_weight, conv_bias, tile_values, tile_cols, tile_count, cheb_weight, cheb_bias
):
    row_count, flat_width = inputs.shape
    chan_in = conv_weight.shape[1]
    chan_out = cheb_weight.shape[2]
    steps_dev = flat_width // chan_in
    block_count, block_rows = (tile_values.shape[0], tile_values.shape[2])
    feat_width = steps_dev * chan_out
    earlier = passed_along(inputs, "tm", 1)
    window = jnp.concatenate([earlier, inputs], axis=1)
    wpair = pair_weight(conv_weight)
    pair_w = 2 * chan_in
    pieces = []
    for p in range(steps_dev // 2):
        base = steps_dev * chan_in + p * pair_w
        newest = window[:, base : base + pair_w]
        middle = window[:, base - pair_w : base]
        oldest = window[:, base - 2 * pair_w : base - pair_w]
        lhs = jnp.concatenate([newest, middle, oldest, newest], axis=1)
        mixed = jnp.dot(lhs, wpair, preferred_element_type=jnp.float32)
        for tt in range(2):
            lo = tt * 2 * chan_out
            linear = mixed[:, lo : lo + chan_out] + conv_bias[:chan_out]
            gate = mixed[:, lo + chan_out : lo + 2 * chan_out] + conv_bias[chan_out:]
            pieces.append(linear * jax.nn.sigmoid(gate))
    flat_features = jnp.concatenate(pieces, axis=1).astype(jnp.bfloat16)
    first_block = lax.axis_index("node") * block_count

    band_tiles = build_band(tile_values, tile_cols, tile_count, first_block)
    node_count = lax.axis_size("node")
    to_right = [(i, i + 1) for i in range(node_count - 1)]
    to_left = [(i + 1, i) for i in range(node_count - 1)]
    rim = HB * block_rows
    feat_left = lax.ppermute(flat_features[row_count - rim :], "node", to_right)
    feat_right = lax.ppermute(flat_features[:rim], "node", to_left)
    order_one = first_product(band_tiles, feat_left, flat_features, feat_right)
    one_left = lax.ppermute(order_one[row_count - rim :], "node", to_right)
    one_right = lax.ppermute(order_one[:rim], "node", to_left)
    result = second_product(
        band_tiles, one_left, order_one, one_right, flat_features, cheb_weight, cheb_bias
    )
    return result.reshape(row_count, steps_dev, chan_out)


def solution(mesh):
    placed = (
        P("node", "tm"),
        P(),
        P(),
        P("node", None, None, None),
        P("node", None),
        P("node"),
        P(),
        P(),
    )
    return jax.shard_map(
        shards, mesh=mesh, in_specs=placed, out_specs=P("node", "tm", None), check_vma=False
    )
```

```python
import jax
import jax.numpy as jnp
from jax import lax
from jax.sharding import PartitionSpec as P
from jax.experimental import pallas as pl
from jax.experimental.pallas import tpu as pltpu

HB = 2
TPB = 4


def with_halo(cells, sides, width):
    for axis, dim in sides:
        count = lax.axis_size(axis)
        ends = count - 1
        head = lax.slice_in_dim(cells, 0, width, axis=dim)
        tail = lax.slice_in_dim(cells, cells.shape[dim] - width, cells.shape[dim], axis=dim)
        cells = jnp.concatenate(
            [
                lax.ppermute(tail, axis, [(i, (i + 1) % count) for i in range(ends)]),
                cells,
                lax.ppermute(head, axis, [((i + 1) % count, i) for i in range(ends)]),
            ],
            axis=dim,
        )
    return cells


def passed_along(value, axis, by):
    length = lax.axis_size(axis)
    pairs = [(i, i + by) for i in range(length) if 0 <= i + by < length]
    return lax.ppermute(value, axis, pairs)


def build_band(tile_set, col_ids, live_count, first_block):
    block_count = tile_set.shape[0]
    row_ids = first_block + jnp.arange(block_count, dtype=jnp.int32)
    offset = col_ids - row_ids[:, None] + HB
    live_mask = jnp.arange(TPB, dtype=jnp.int32)[None, :] < live_count[:, None]
    tiles = tile_set.astype(jnp.float32)
    parts = []
    for o in range(2 * HB + 1):
        pick = ((offset == o) & live_mask).astype(jnp.float32)
        parts.append(jnp.sum(pick[:, :, None, None] * tiles, axis=1))
    return jnp.concatenate(parts, axis=2).astype(jnp.bfloat16)


def band_product(band_tiles, extended):
    block_count = band_tiles.shape[0]
    total = jnp.einsum(
        "bpq,bqf->bpf",
        band_tiles[:, 0],
        extended[0:block_count],
        preferred_element_type=jnp.float32,
    )
    for offset in range(1, 2 * HB + 1):
        total = total + jnp.einsum(
            "bpq,bqf->bpf",
            band_tiles[:, offset],
            extended[offset : offset + block_count],
            preferred_element_type=jnp.float32,
        )
    return total


def _assemble(ext_ref, left_ref, own_ref, right_ref):
    rim = left_ref.shape[0]
    rows = own_ref.shape[0]
    ext_ref[0:rim, :] = left_ref[...]
    ext_ref[rim : rim + rows, :] = own_ref[...]
    ext_ref[rim + rows : 2 * rim + rows, :] = right_ref[...]


def _band_block(b, band_ref, ext_ref):
    rows = band_ref.shape[1]
    reach = band_ref.shape[2]
    return jnp.dot(
        band_ref[b], ext_ref[b * rows : b * rows + reach, :], preferred_element_type=jnp.float32
    )


def _first_kernel(band_ref, left_ref, own_ref, right_ref, out_ref, ext_ref):
    nb, rows = band_ref.shape[0], band_ref.shape[1]
    _assemble(ext_ref, left_ref, own_ref, right_ref)
    for b in range(nb):
        out_ref[b * rows : (b + 1) * rows, :] = _band_block(b, band_ref, ext_ref).astype(out_ref.dtype)


def _second_kernel(
    band_ref, left_ref, own_ref, right_ref, feat_ref, weight_ref, bias_ref, out_ref, ext_ref, two_ref
):
    nb, rows = band_ref.shape[0], band_ref.shape[1]
    chan = weight_ref.shape[1]
    steps = own_ref.shape[1] // chan
    _assemble(ext_ref, left_ref, own_ref, right_ref)
    for b in range(nb):
        lo, hi = b * rows, (b + 1) * rows
        acc = _band_block(b, band_ref, ext_ref)
        two_ref[lo:hi, :] = (2.0 * acc - feat_ref[lo:hi, :].astype(jnp.float32)).astype(two_ref.dtype)
    bias = bias_ref[...]
    for t in range(steps):
        cols = slice(t * chan, (t + 1) * chan)
        joined = jnp.concatenate([feat_ref[:, cols], own_ref[:, cols], two_ref[:, cols]], axis=1)
        res = jnp.dot(joined, weight_ref[...], preferred_element_type=jnp.float32) + bias
        out_ref[:, cols] = jnp.maximum(res, 0.0).astype(out_ref.dtype)


def _vmem_specs(count):
    return [pl.BlockSpec(memory_space=pltpu.VMEM) for _ in range(count)]


def first_product(band_tiles, left, own, right):
    rows, width = own.shape
    flops = 2 * band_tiles.shape[0] * band_tiles.shape[1] * band_tiles.shape[2] * width
    return pl.pallas_call(
        _first_kernel,
        out_shape=jax.ShapeDtypeStruct((rows, width), jnp.bfloat16),
        in_specs=_vmem_specs(4),
        out_specs=pl.BlockSpec(memory_space=pltpu.VMEM),
        scratch_shapes=[pltpu.VMEM((rows + 2 * left.shape[0], width), own.dtype)],
        cost_estimate=pl.CostEstimate(flops=flops, transcendentals=0, bytes_accessed=6 * rows * width),
    )(band_tiles, left, own, right)


def second_product(band_tiles, left, own, right, features, cheb_weight, cheb_bias):
    rows, width = own.shape
    weight = cheb_weight.reshape(-1, cheb_weight.shape[2])
    bias = cheb_bias.reshape(1, -1)
    flops = 2 * band_tiles.shape[0] * band_tiles.shape[1] * band_tiles.shape[2] * width
    flops += 2 * rows * width * weight.shape[0]
    return pl.pallas_call(
        _second_kernel,
        out_shape=jax.ShapeDtypeStruct((rows, width), jnp.bfloat16),
        in_specs=_vmem_specs(7),
        out_specs=pl.BlockSpec(memory_space=pltpu.VMEM),
        scratch_shapes=[
            pltpu.VMEM((rows + 2 * left.shape[0], width), own.dtype),
            pltpu.VMEM((rows, width), jnp.bfloat16),
        ],
        cost_estimate=pl.CostEstimate(flops=flops, transcendentals=0, bytes_accessed=8 * rows * width),
    )(band_tiles, left, own, right, features, weight, bias)

def fetch_rim(values, block_rows):
    return with_halo(values, (("node", 0),), HB * block_rows)


def pair_weight(conv_weight):
    taps, chan_in, width = conv_weight.shape
    eye = jnp.eye(2, dtype=conv_weight.dtype)
    blocks = [jnp.kron(eye, conv_weight[k]) for k in range(taps)]
    rows_in = jnp.arange(2 * chan_in, dtype=jnp.int32)[:, None]
    cols_out = jnp.arange(2 * width, dtype=jnp.int32)[None, :]
    place = (cols_out == rows_in // chan_in * width + rows_in % chan_in).astype(conv_weight.dtype)
    return jnp.concatenate(blocks + [place], axis=0)


def block_diag(weight, steps):
    return jnp.kron(jnp.eye(steps, dtype=weight.dtype), weight)


def shards(
    inputs, conv_weight, conv_bias, tile_values, tile_cols, tile_count, cheb_weight, cheb_bias
):
    row_count, flat_width = inputs.shape
    chan_in = conv_weight.shape[1]
    chan_out = cheb_weight.shape[2]
    steps_dev = flat_width // chan_in
    block_count, block_rows = (tile_values.shape[0], tile_values.shape[2])
    feat_width = steps_dev * chan_out
    earlier = passed_along(inputs, "tm", 1)
    window = jnp.concatenate([earlier, inputs], axis=1)
    wpair = pair_weight(conv_weight)
    pair_w = 2 * chan_in
    pieces = []
    for p in range(steps_dev // 2):
        base = steps_dev * chan_in + p * pair_w
        newest = window[:, base : base + pair_w]
        middle = window[:, base - pair_w : base]
        oldest = window[:, base - 2 * pair_w : base - pair_w]
        lhs = jnp.concatenate([newest, middle, oldest, newest], axis=1)
        mixed = jnp.dot(lhs, wpair, preferred_element_type=jnp.float32)
        for tt in range(2):
            lo = tt * 2 * chan_out
            linear = mixed[:, lo : lo + chan_out] + conv_bias[:chan_out]
            gate = mixed[:, lo + chan_out : lo + 2 * chan_out] + conv_bias[chan_out:]
            pieces.append(linear * jax.nn.sigmoid(gate))
    flat_features = jnp.concatenate(pieces, axis=1).astype(jnp.bfloat16)
    first_block = lax.axis_index("node") * block_count

    band_tiles = build_band(tile_values, tile_cols, tile_count, first_block)
    node_count = lax.axis_size("node")
    to_right = [(i, i + 1) for i in range(node_count - 1)]
    to_left = [(i + 1, i) for i in range(node_count - 1)]
    rim = HB * block_rows
    feat_left = lax.ppermute(flat_features[row_count - rim :], "node", to_right)
    feat_right = lax.ppermute(flat_features[:rim], "node", to_left)
    order_one = first_product(band_tiles, feat_left, flat_features, feat_right)
    one_left = lax.ppermute(order_one[row_count - rim :], "node", to_right)
    one_right = lax.ppermute(order_one[:rim], "node", to_left)
    result = second_product(
        band_tiles, one_left, order_one, one_right, flat_features, cheb_weight, cheb_bias
    )
    return result.reshape(row_count, steps_dev, chan_out)


def solution(mesh):
    placed = (
        P("node", "tm"),
        P(),
        P(),
        P("node", None, None, None),
        P("node", None),
        P("node"),
        P(),
        P(),
    )
    return jax.shard_map(
        shards, mesh=mesh, in_specs=placed, out_specs=P("node", "tm", None), check_vma=False
    )
```

```python
import jax
import jax.numpy as jnp
from jax import lax
from jax.sharding import PartitionSpec as P

HB = 2
TPB = 4


def with_halo(cells, sides, width):
    for axis, dim in sides:
        count = lax.axis_size(axis)
        ends = count - 1
        head = lax.slice_in_dim(cells, 0, width, axis=dim)
        tail = lax.slice_in_dim(cells, cells.shape[dim] - width, cells.shape[dim], axis=dim)
        cells = jnp.concatenate(
            [
                lax.ppermute(tail, axis, [(i, (i + 1) % count) for i in range(ends)]),
                cells,
                lax.ppermute(head, axis, [((i + 1) % count, i) for i in range(ends)]),
            ],
            axis=dim,
        )
    return cells


def passed_along(value, axis, by):
    length = lax.axis_size(axis)
    pairs = [(i, i + by) for i in range(length) if 0 <= i + by < length]
    return lax.ppermute(value, axis, pairs)


def build_band(tile_set, col_ids, live_count, first_block):
    block_count = tile_set.shape[0]
    row_ids = first_block + jnp.arange(block_count, dtype=jnp.int32)
    offset = col_ids - row_ids[:, None] + HB
    live_mask = jnp.arange(TPB, dtype=jnp.int32)[None, :] < live_count[:, None]
    one_hot = (
        offset[:, :, None] == jnp.arange(2 * HB + 1, dtype=jnp.int32)[None, None, :]
    ) & live_mask[:, :, None]
    band_tiles = jnp.einsum(
        "bjo,bjpq->bopq", one_hot.astype(jnp.bfloat16), tile_set, preferred_element_type=jnp.float32
    )
    return band_tiles.astype(jnp.bfloat16)


def band_product(band_tiles, extended):
    block_count = band_tiles.shape[0]
    total = jnp.einsum(
        "bpq,bqf->bpf",
        band_tiles[:, 0],
        extended[0:block_count],
        preferred_element_type=jnp.float32,
    )
    for offset in range(1, 2 * HB + 1):
        total = total + jnp.einsum(
            "bpq,bqf->bpf",
            band_tiles[:, offset],
            extended[offset : offset + block_count],
            preferred_element_type=jnp.float32,
        )
    return total


def fetch_rim(values, block_rows):
    return with_halo(values, (("node", 0),), HB * block_rows)


def pair_weight(conv_weight):
    taps, chan_in, width = conv_weight.shape
    eye = jnp.eye(2, dtype=conv_weight.dtype)
    blocks = [jnp.kron(eye, conv_weight[k]) for k in range(taps)]
    rows_in = jnp.arange(2 * chan_in, dtype=jnp.int32)[:, None]
    cols_out = jnp.arange(2 * width, dtype=jnp.int32)[None, :]
    place = (cols_out == rows_in // chan_in * width + rows_in % chan_in).astype(conv_weight.dtype)
    return jnp.concatenate(blocks + [place], axis=0)


def block_diag(weight, steps):
    return jnp.kron(jnp.eye(steps, dtype=weight.dtype), weight)


def shards(
    inputs, conv_weight, conv_bias, tile_values, tile_cols, tile_count, cheb_weight, cheb_bias
):
    row_count, flat_width = inputs.shape
    chan_in = conv_weight.shape[1]
    chan_out = cheb_weight.shape[2]
    steps_dev = flat_width // chan_in
    block_count, block_rows = (tile_values.shape[0], tile_values.shape[2])
    feat_width = steps_dev * chan_out
    earlier = passed_along(inputs, "tm", 1)
    window = jnp.concatenate([earlier, inputs], axis=1)
    wpair = pair_weight(conv_weight)
    rim = HB * block_rows

    def conv(rows):
        pair_w = 2 * chan_in
        pieces = []
        for p in range(steps_dev // 2):
            base = steps_dev * chan_in + p * pair_w
            newest = rows[:, base : base + pair_w]
            middle = rows[:, base - pair_w : base]
            oldest = rows[:, base - 2 * pair_w : base - pair_w]
            lhs = jnp.concatenate([newest, middle, oldest, newest], axis=1)
            mixed = jnp.dot(lhs, wpair, preferred_element_type=jnp.float32)
            for tt in range(2):
                lo = tt * 2 * chan_out
                linear = mixed[:, lo : lo + chan_out] + conv_bias[:chan_out]
                gate = mixed[:, lo + chan_out : lo + 2 * chan_out] + conv_bias[chan_out:]
                pieces.append(linear * jax.nn.sigmoid(gate))
        return jnp.concatenate(pieces, axis=1).astype(jnp.bfloat16)

    node_count = lax.axis_size("node")
    to_right = [(i, i + 1) for i in range(node_count - 1)]
    to_left = [(i + 1, i) for i in range(node_count - 1)]
    feat_head = conv(window[:rim])
    feat_tail = conv(window[row_count - rim :])
    feat_left = lax.ppermute(feat_tail, "node", to_right)
    feat_right = lax.ppermute(feat_head, "node", to_left)
    feat_mid = conv(window[rim : row_count - rim])
    flat_features = jnp.concatenate([feat_head, feat_mid, feat_tail], axis=0)
    first_block = lax.axis_index("node") * block_count
    band_tiles = build_band(tile_values, tile_cols, tile_count, first_block)

    def blocks(*parts):
        joined = jnp.concatenate(parts, axis=0) if len(parts) > 1 else parts[0]
        return joined.reshape(-1, block_rows, feat_width)

    def edges(band, left, own, right):
        head = band_product(band[:HB], blocks(left, own[: 2 * rim]))
        tail = band_product(band[block_count - HB :], blocks(own[row_count - 2 * rim :], right))
        return head.reshape(rim, feat_width), tail.reshape(rim, feat_width)

    one_head, one_tail = edges(band_tiles, feat_left, flat_features, feat_right)
    one_head = one_head.astype(jnp.bfloat16)
    one_tail = one_tail.astype(jnp.bfloat16)
    one_left = lax.ppermute(one_tail, "node", to_right)
    one_right = lax.ppermute(one_head, "node", to_left)
    one_mid = band_product(band_tiles[HB : block_count - HB], blocks(flat_features))
    one_mid = one_mid.reshape(row_count - 2 * rim, feat_width).astype(jnp.bfloat16)
    order_one = jnp.concatenate([one_head, one_mid, one_tail], axis=0)

    kron = [block_diag(cheb_weight[k], steps_dev) for k in range(3)]
    early = jnp.dot(
        jnp.concatenate([flat_features, order_one], axis=1),
        jnp.concatenate(kron[:2], axis=0),
        preferred_element_type=jnp.float32,
    ) + jnp.tile(cheb_bias, steps_dev)

    def finish(two, feat, part):
        cheb_two = (2.0 * two - feat.astype(jnp.float32)).astype(jnp.bfloat16)
        return part + jnp.dot(cheb_two, kron[2], preferred_element_type=jnp.float32)

    two_mid = band_product(band_tiles[HB : block_count - HB], blocks(order_one))
    two_mid = two_mid.reshape(row_count - 2 * rim, feat_width)
    res_mid = finish(two_mid, feat_mid, early[rim : row_count - rim])
    two_head, two_tail = edges(band_tiles, one_left, order_one, one_right)
    res_head = finish(two_head, feat_head, early[:rim])
    res_tail = finish(two_tail, feat_tail, early[row_count - rim :])
    result = jnp.concatenate([res_head, res_mid, res_tail], axis=0)
    return jax.nn.relu(result).astype(jnp.bfloat16).reshape(row_count, steps_dev, chan_out)

def solution(mesh):
    placed = (
        P("node", "tm"),
        P(),
        P(),
        P("node", None, None, None),
        P("node", None),
        P("node"),
        P(),
        P(),
    )
    return jax.shard_map(
        shards, mesh=mesh, in_specs=placed, out_specs=P("node", "tm", None), check_vma=False
    )
```

```python
import jax
import jax.numpy as jnp
from jax import lax
from jax.sharding import PartitionSpec as P

HB = 2
TPB = 4


def with_halo(cells, sides, width):
    for axis, dim in sides:
        count = lax.axis_size(axis)
        ends = count - 1
        head = lax.slice_in_dim(cells, 0, width, axis=dim)
        tail = lax.slice_in_dim(cells, cells.shape[dim] - width, cells.shape[dim], axis=dim)
        cells = jnp.concatenate(
            [
                lax.ppermute(tail, axis, [(i, (i + 1) % count) for i in range(ends)]),
                cells,
                lax.ppermute(head, axis, [((i + 1) % count, i) for i in range(ends)]),
            ],
            axis=dim,
        )
    return cells


def passed_along(value, axis, by):
    length = lax.axis_size(axis)
    pairs = [(i, i + by) for i in range(length) if 0 <= i + by < length]
    return lax.ppermute(value, axis, pairs)


def build_band(tile_set, col_ids, live_count, first_block):
    block_count = tile_set.shape[0]
    row_ids = first_block + jnp.arange(block_count, dtype=jnp.int32)
    offset = col_ids - row_ids[:, None] + HB
    live_mask = jnp.arange(TPB, dtype=jnp.int32)[None, :] < live_count[:, None]
    one_hot = (
        offset[:, :, None] == jnp.arange(2 * HB + 1, dtype=jnp.int32)[None, None, :]
    ) & live_mask[:, :, None]
    band_tiles = jnp.einsum(
        "bjo,bjpq->bopq", one_hot.astype(jnp.bfloat16), tile_set, preferred_element_type=jnp.float32
    )
    return band_tiles.astype(jnp.bfloat16)


def band_product(band_tiles, extended):
    block_count = band_tiles.shape[0]
    total = jnp.einsum(
        "bpq,bqf->bpf",
        band_tiles[:, 0],
        extended[0:block_count],
        preferred_element_type=jnp.float32,
    )
    for offset in range(1, 2 * HB + 1):
        total = total + jnp.einsum(
            "bpq,bqf->bpf",
            band_tiles[:, offset],
            extended[offset : offset + block_count],
            preferred_element_type=jnp.float32,
        )
    return total


def fetch_rim(values, block_rows):
    return with_halo(values, (("node", 0),), HB * block_rows)


def pair_weight(conv_weight):
    taps, chan_in, width = conv_weight.shape
    eye = jnp.eye(2, dtype=conv_weight.dtype)
    blocks = [jnp.kron(eye, conv_weight[k]) for k in range(taps)]
    rows_in = jnp.arange(2 * chan_in, dtype=jnp.int32)[:, None]
    cols_out = jnp.arange(2 * width, dtype=jnp.int32)[None, :]
    place = (cols_out == rows_in // chan_in * width + rows_in % chan_in).astype(conv_weight.dtype)
    return jnp.concatenate(blocks + [place], axis=0)


def block_diag(weight, steps):
    return jnp.kron(jnp.eye(steps, dtype=weight.dtype), weight)


def shards(
    inputs, conv_weight, conv_bias, tile_values, tile_cols, tile_count, cheb_weight, cheb_bias
):
    row_count, flat_width = inputs.shape
    chan_in = conv_weight.shape[1]
    chan_out = cheb_weight.shape[2]
    steps_dev = flat_width // chan_in
    block_count, block_rows = (tile_values.shape[0], tile_values.shape[2])
    feat_width = steps_dev * chan_out
    earlier = passed_along(inputs, "tm", 1)
    window = jnp.concatenate([earlier, inputs], axis=1)
    wpair = pair_weight(conv_weight)
    pair_w = 2 * chan_in
    pieces = []
    for p in range(steps_dev // 2):
        base = steps_dev * chan_in + p * pair_w
        newest = window[:, base : base + pair_w]
        middle = window[:, base - pair_w : base]
        oldest = window[:, base - 2 * pair_w : base - pair_w]
        lhs = jnp.concatenate([newest, middle, oldest, newest], axis=1)
        mixed = jnp.dot(lhs, wpair, preferred_element_type=jnp.float32)
        for tt in range(2):
            lo = tt * 2 * chan_out
            linear = mixed[:, lo : lo + chan_out] + conv_bias[:chan_out]
            gate = mixed[:, lo + chan_out : lo + 2 * chan_out] + conv_bias[chan_out:]
            pieces.append(linear * jax.nn.sigmoid(gate))
    flat_features = jnp.concatenate(pieces, axis=1).astype(jnp.bfloat16)
    first_block = lax.axis_index("node") * block_count
    band_tiles = build_band(tile_values, tile_cols, tile_count, first_block)
    node_count = lax.axis_size("node")
    to_right = [(i, i + 1) for i in range(node_count - 1)]
    to_left = [(i + 1, i) for i in range(node_count - 1)]
    rim = HB * block_rows
    edge_ids = list(range(HB)) + list(range(block_count - HB, block_count))
    halo_band = []
    for b in edge_ids:
        terms = []
        for o in range(2 * HB + 1):
            j = b + o
            if j < HB or j >= block_count + HB:
                terms.append(band_tiles[b, o])
        while len(terms) < HB:
            terms.append(jnp.zeros_like(band_tiles[0, 0]))
        halo_band.append(jnp.stack(terms))
    halo_band = jnp.stack(halo_band)

    def halo_blocks(left, right):
        lb = left.reshape(HB, block_rows, feat_width)
        rb = right.reshape(HB, block_rows, feat_width)
        picks = []
        for b in edge_ids:
            terms = []
            for o in range(2 * HB + 1):
                j = b + o
                if j < HB:
                    terms.append(lb[j])
                elif j >= block_count + HB:
                    terms.append(rb[j - block_count - HB])
            while len(terms) < HB:
                terms.append(terms[-1])
            picks.append(jnp.stack(terms))
        return jnp.stack(picks)

    def halo_part(left, right):
        part = jnp.einsum(
            "bkpq,bkqf->bpf", halo_band, halo_blocks(left, right), preferred_element_type=jnp.float32
        )
        middle = jnp.zeros((block_count - 2 * HB, block_rows, feat_width), jnp.float32)
        return jnp.concatenate([part[:HB], middle, part[HB:]], axis=0)

    def own_part(values):
        padded = jnp.pad(values.reshape(block_count, block_rows, feat_width), ((HB, HB), (0, 0), (0, 0)))
        return band_product(band_tiles, padded)

    feat_left = lax.ppermute(flat_features[row_count - rim :], "node", to_right)
    feat_right = lax.ppermute(flat_features[:rim], "node", to_left)
    one_own = own_part(flat_features)
    order_one = (one_own + halo_part(feat_left, feat_right)).astype(jnp.bfloat16)
    order_one = order_one.reshape(row_count, feat_width)
    one_left = lax.ppermute(order_one[row_count - rim :], "node", to_right)
    one_right = lax.ppermute(order_one[:rim], "node", to_left)
    two_own = own_part(order_one)
    kron = [block_diag(cheb_weight[k], steps_dev) for k in range(3)]
    early = jnp.dot(
        jnp.concatenate([flat_features, order_one], axis=1),
        jnp.concatenate(kron[:2], axis=0),
        preferred_element_type=jnp.float32,
    ) + jnp.tile(cheb_bias, steps_dev)
    order_two = (two_own + halo_part(one_left, one_right)).reshape(row_count, feat_width)
    cheb_two = (2.0 * order_two - flat_features.astype(jnp.float32)).astype(jnp.bfloat16)
    result = early + jnp.dot(cheb_two, kron[2], preferred_element_type=jnp.float32)
    return jax.nn.relu(result).astype(jnp.bfloat16).reshape(row_count, steps_dev, chan_out)

def solution(mesh):
    placed = (
        P("node", "tm"),
        P(),
        P(),
        P("node", None, None, None),
        P("node", None),
        P("node"),
        P(),
        P(),
    )
    return jax.shard_map(
        shards, mesh=mesh, in_specs=placed, out_specs=P("node", "tm", None), check_vma=False
    )
```

```python
import jax
import jax.numpy as jnp
from jax import lax
from jax.sharding import PartitionSpec as P

HB = 2
TPB = 4


def passed_along(value, axis, by):
    length = lax.axis_size(axis)
    pairs = [(i, i + by) for i in range(length) if 0 <= i + by < length]
    return lax.ppermute(value, axis, pairs)


def build_band(tile_set, col_ids, live_count, first_block):
    block_count = tile_set.shape[0]
    row_ids = first_block + jnp.arange(block_count, dtype=jnp.int32)
    offset = col_ids - row_ids[:, None] + HB
    live_mask = jnp.arange(TPB, dtype=jnp.int32)[None, :] < live_count[:, None]
    one_hot = (
        offset[:, :, None] == jnp.arange(2 * HB + 1, dtype=jnp.int32)[None, None, :]
    ) & live_mask[:, :, None]
    band_tiles = jnp.einsum(
        "bjo,bjpq->bopq", one_hot.astype(jnp.bfloat16), tile_set, preferred_element_type=jnp.float32
    )
    return band_tiles.astype(jnp.bfloat16)


def band_product(band_tiles, extended):
    block_count = band_tiles.shape[0]
    total = jnp.einsum(
        "bpq,bqf->bpf",
        band_tiles[:, 0],
        extended[0:block_count],
        preferred_element_type=jnp.float32,
    )
    for offset in range(1, 2 * HB + 1):
        total = total + jnp.einsum(
            "bpq,bqf->bpf",
            band_tiles[:, offset],
            extended[offset : offset + block_count],
            preferred_element_type=jnp.float32,
        )
    return total


def pair_weight(conv_weight):
    taps, chan_in, width = conv_weight.shape
    eye = jnp.eye(2, dtype=conv_weight.dtype)
    blocks = [jnp.kron(eye, conv_weight[k]) for k in range(taps)]
    rows_in = jnp.arange(2 * chan_in, dtype=jnp.int32)[:, None]
    cols_out = jnp.arange(2 * width, dtype=jnp.int32)[None, :]
    place = (cols_out == rows_in // chan_in * width + rows_in % chan_in).astype(conv_weight.dtype)
    return jnp.concatenate(blocks + [place], axis=0)


def block_diag(weight, steps):
    return jnp.kron(jnp.eye(steps, dtype=weight.dtype), weight)


def stage(
    inputs, conv_weight, conv_bias, tile_values, tile_cols, tile_count, cheb_weight, cheb_bias
):
    row_count, flat_width = inputs.shape
    chan_in = conv_weight.shape[1]
    chan_out = cheb_weight.shape[2]
    steps_dev = flat_width // chan_in
    block_count, block_rows = (tile_values.shape[0], tile_values.shape[2])
    feat_width = steps_dev * chan_out
    rim = HB * block_rows
    wpair = pair_weight(conv_weight)

    def conv(window):
        pair_w = 2 * chan_in
        pieces = []
        for p in range(steps_dev // 2):
            base = steps_dev * chan_in + p * pair_w
            newest = window[:, base : base + pair_w]
            middle = window[:, base - pair_w : base]
            oldest = window[:, base - 2 * pair_w : base - pair_w]
            lhs = jnp.concatenate([newest, middle, oldest, newest], axis=1)
            mixed = jnp.dot(lhs, wpair, preferred_element_type=jnp.float32)
            for tt in range(2):
                lo = tt * 2 * chan_out
                linear = mixed[:, lo : lo + chan_out] + conv_bias[:chan_out]
                gate = mixed[:, lo + chan_out : lo + 2 * chan_out] + conv_bias[chan_out:]
                pieces.append(linear * jax.nn.sigmoid(gate))
        return jnp.concatenate(pieces, axis=1).astype(jnp.bfloat16)

    edge_in = jnp.concatenate([inputs[:rim], inputs[row_count - rim :]], axis=0)
    mid_in = inputs[rim : row_count - rim]
    edge_prev = passed_along(edge_in, "tm", 1)
    mid_prev = passed_along(mid_in, "tm", 1)
    feat_edge = conv(jnp.concatenate([edge_prev, edge_in], axis=1))
    feat_head = feat_edge[:rim]
    feat_tail = feat_edge[rim:]
    first_block = lax.axis_index("node") * block_count
    band_tiles = build_band(tile_values, tile_cols, tile_count, first_block)
    node_count = lax.axis_size("node")
    to_right = [(i, i + 1) for i in range(node_count - 1)]
    to_left = [(i + 1, i) for i in range(node_count - 1)]
    edge_ids = list(range(HB)) + list(range(block_count - HB, block_count))
    halo_band = []
    for b in edge_ids:
        terms = []
        for o in range(2 * HB + 1):
            j = b + o
            if j < HB or j >= block_count + HB:
                terms.append(band_tiles[b, o])
        while len(terms) < HB:
            terms.append(jnp.zeros_like(band_tiles[0, 0]))
        halo_band.append(jnp.stack(terms))
    halo_band = jnp.stack(halo_band)

    def halo_blocks(left, right):
        lb = left.reshape(HB, block_rows, feat_width)
        rb = right.reshape(HB, block_rows, feat_width)
        picks = []
        for b in edge_ids:
            terms = []
            for o in range(2 * HB + 1):
                j = b + o
                if j < HB:
                    terms.append(lb[j])
                elif j >= block_count + HB:
                    terms.append(rb[j - block_count - HB])
            while len(terms) < HB:
                terms.append(terms[-1])
            picks.append(jnp.stack(terms))
        return jnp.stack(picks)

    def halo_part(left, right):
        part = jnp.einsum(
            "bkpq,bkqf->bpf", halo_band, halo_blocks(left, right), preferred_element_type=jnp.float32
        )
        middle = jnp.zeros((block_count - 2 * HB, block_rows, feat_width), jnp.float32)
        return jnp.concatenate([part[:HB], middle, part[HB:]], axis=0)

    def own_part(values):
        padded = jnp.pad(values.reshape(block_count, block_rows, feat_width), ((HB, HB), (0, 0), (0, 0)))
        return band_product(band_tiles, padded)

    feat_left = lax.ppermute(feat_tail, "node", to_right)
    feat_right = lax.ppermute(feat_head, "node", to_left)
    mid_window, _ = lax.optimization_barrier(
        (jnp.concatenate([mid_prev, mid_in], axis=1), feat_edge)
    )
    feat_mid = conv(mid_window)
    flat_features = jnp.concatenate([feat_head, feat_mid, feat_tail], axis=0)
    one_own = own_part(flat_features)
    order_one = (one_own + halo_part(feat_left, feat_right)).astype(jnp.bfloat16)
    order_one = order_one.reshape(row_count, feat_width)
    one_left = lax.ppermute(order_one[row_count - rim :], "node", to_right)
    one_right = lax.ppermute(order_one[:rim], "node", to_left)
    two_own = own_part(order_one)
    kron = [block_diag(cheb_weight[k], steps_dev) for k in range(3)]
    early = jnp.dot(
        jnp.concatenate([flat_features, order_one], axis=1),
        jnp.concatenate(kron[:2], axis=0),
        preferred_element_type=jnp.float32,
    ) + jnp.tile(cheb_bias, steps_dev)
    order_two = (two_own + halo_part(one_left, one_right)).reshape(row_count, feat_width)
    cheb_two = (2.0 * order_two - flat_features.astype(jnp.float32)).astype(jnp.bfloat16)
    result = early + jnp.dot(cheb_two, kron[2], preferred_element_type=jnp.float32)
    return jax.nn.relu(result).astype(jnp.bfloat16).reshape(row_count, steps_dev, chan_out)


def solution(mesh):
    placed = (
        P("node", "tm"),
        P(),
        P(),
        P("node", None, None, None),
        P("node", None),
        P("node"),
        P(),
        P(),
    )
    return jax.shard_map(
        stage, mesh=mesh, in_specs=placed, out_specs=P("node", "tm", None), check_vma=False
    )
```

```python
import jax
import jax.numpy as jnp
from jax import lax
from jax.sharding import PartitionSpec as P

HB = 2
TPB = 4


def passed_along(value, axis, by):
    length = lax.axis_size(axis)
    pairs = [(i, i + by) for i in range(length) if 0 <= i + by < length]
    return lax.ppermute(value, axis, pairs)


def build_band(tile_set, col_ids, live_count, first_block):
    block_count = tile_set.shape[0]
    row_ids = first_block + jnp.arange(block_count, dtype=jnp.int32)
    offset = col_ids - row_ids[:, None] + HB
    live_mask = jnp.arange(TPB, dtype=jnp.int32)[None, :] < live_count[:, None]
    one_hot = (
        offset[:, :, None] == jnp.arange(2 * HB + 1, dtype=jnp.int32)[None, None, :]
    ) & live_mask[:, :, None]
    band_tiles = jnp.einsum(
        "bjo,bjpq->bopq", one_hot.astype(jnp.bfloat16), tile_set, preferred_element_type=jnp.float32
    )
    return band_tiles.astype(jnp.bfloat16)


def band_product(band_tiles, extended):
    block_count = band_tiles.shape[0]
    total = jnp.einsum(
        "bpq,bqf->bpf",
        band_tiles[:, 0],
        extended[0:block_count],
        preferred_element_type=jnp.float32,
    )
    for offset in range(1, 2 * HB + 1):
        total = total + jnp.einsum(
            "bpq,bqf->bpf",
            band_tiles[:, offset],
            extended[offset : offset + block_count],
            preferred_element_type=jnp.float32,
        )
    return total


def pair_weight(conv_weight):
    taps, chan_in, width = conv_weight.shape
    eye = jnp.eye(2, dtype=conv_weight.dtype)
    blocks = [jnp.kron(eye, conv_weight[k]) for k in range(taps)]
    rows_in = jnp.arange(2 * chan_in, dtype=jnp.int32)[:, None]
    cols_out = jnp.arange(2 * width, dtype=jnp.int32)[None, :]
    place = (cols_out == rows_in // chan_in * width + rows_in % chan_in).astype(conv_weight.dtype)
    return jnp.concatenate(blocks + [place], axis=0)


def block_diag(weight, steps):
    return jnp.kron(jnp.eye(steps, dtype=weight.dtype), weight)


def stage(
    inputs, conv_weight, conv_bias, tile_values, tile_cols, tile_count, cheb_weight, cheb_bias
):
    row_count, flat_width = inputs.shape
    chan_in = conv_weight.shape[1]
    chan_out = cheb_weight.shape[2]
    steps_dev = flat_width // chan_in
    block_count, block_rows = (tile_values.shape[0], tile_values.shape[2])
    feat_width = steps_dev * chan_out
    earlier = passed_along(inputs, "tm", 1)
    window = jnp.concatenate([earlier, inputs], axis=1)
    wpair = pair_weight(conv_weight)
    pair_w = 2 * chan_in
    pieces = []
    for p in range(steps_dev // 2):
        base = steps_dev * chan_in + p * pair_w
        newest = window[:, base : base + pair_w]
        middle = window[:, base - pair_w : base]
        oldest = window[:, base - 2 * pair_w : base - pair_w]
        lhs = jnp.concatenate([newest, middle, oldest, newest], axis=1)
        mixed = jnp.dot(lhs, wpair, preferred_element_type=jnp.float32)
        for tt in range(2):
            lo = tt * 2 * chan_out
            linear = mixed[:, lo : lo + chan_out] + conv_bias[:chan_out]
            gate = mixed[:, lo + chan_out : lo + 2 * chan_out] + conv_bias[chan_out:]
            pieces.append(linear * jax.nn.sigmoid(gate))
    flat_features = jnp.concatenate(pieces, axis=1).astype(jnp.bfloat16)
    first_block = lax.axis_index("node") * block_count
    band_tiles = build_band(tile_values, tile_cols, tile_count, first_block)
    node_count = lax.axis_size("node")
    to_right = [(i, i + 1) for i in range(node_count - 1)]
    to_left = [(i + 1, i) for i in range(node_count - 1)]
    rim = HB * block_rows
    edge_ids = list(range(HB)) + list(range(block_count - HB, block_count))
    halo_band = []
    for b in edge_ids:
        terms = []
        for o in range(2 * HB + 1):
            j = b + o
            if j < HB or j >= block_count + HB:
                terms.append(band_tiles[b, o])
        while len(terms) < HB:
            terms.append(jnp.zeros_like(band_tiles[0, 0]))
        halo_band.append(jnp.stack(terms))
    halo_band = jnp.stack(halo_band)

    def halo_blocks(left, right):
        lb = left.reshape(HB, block_rows, feat_width)
        rb = right.reshape(HB, block_rows, feat_width)
        picks = []
        for b in edge_ids:
            terms = []
            for o in range(2 * HB + 1):
                j = b + o
                if j < HB:
                    terms.append(lb[j])
                elif j >= block_count + HB:
                    terms.append(rb[j - block_count - HB])
            while len(terms) < HB:
                terms.append(terms[-1])
            picks.append(jnp.stack(terms))
        return jnp.stack(picks)

    def halo_part(left, right):
        part = jnp.einsum(
            "bkpq,bkqf->bpf", halo_band, halo_blocks(left, right), preferred_element_type=jnp.float32
        )
        middle = jnp.zeros((block_count - 2 * HB, block_rows, feat_width), jnp.float32)
        return jnp.concatenate([part[:HB], middle, part[HB:]], axis=0)

    def own_part(values):
        padded = jnp.pad(values.reshape(block_count, block_rows, feat_width), ((HB, HB), (0, 0), (0, 0)))
        return band_product(band_tiles, padded)

    feat_left = lax.ppermute(flat_features[row_count - rim :], "node", to_right)
    feat_right = lax.ppermute(flat_features[:rim], "node", to_left)
    one_own = own_part(flat_features)
    order_one = (one_own + halo_part(feat_left, feat_right)).astype(jnp.bfloat16)
    order_one = order_one.reshape(row_count, feat_width)
    one_left = lax.ppermute(order_one[row_count - rim :], "node", to_right)
    one_right = lax.ppermute(order_one[:rim], "node", to_left)
    two_own = own_part(order_one)
    kron = [block_diag(cheb_weight[k], steps_dev) for k in range(3)]
    early = jnp.dot(
        jnp.concatenate([flat_features, order_one], axis=1),
        jnp.concatenate(kron[:2], axis=0),
        preferred_element_type=jnp.float32,
    ) + jnp.tile(cheb_bias, steps_dev)
    order_two = (two_own + halo_part(one_left, one_right)).reshape(row_count, feat_width)
    cheb_two = (2.0 * order_two - flat_features.astype(jnp.float32)).astype(jnp.bfloat16)
    result = early + jnp.dot(cheb_two, kron[2], preferred_element_type=jnp.float32)
    return jax.nn.relu(result).astype(jnp.bfloat16).reshape(row_count, steps_dev, chan_out)


def solution(mesh):
    placed = (
        P("node", "tm"),
        P(),
        P(),
        P("node", None, None, None),
        P("node", None),
        P("node"),
        P(),
        P(),
    )
    return jax.shard_map(
        stage, mesh=mesh, in_specs=placed, out_specs=P("node", "tm", None), check_vma=False
    )
```

```python
import jax
import jax.numpy as jnp
from jax import lax
from jax.sharding import PartitionSpec as P

HB = 2
TPB = 4


def passed_along(value, axis, by):
    length = lax.axis_size(axis)
    pairs = [(i, i + by) for i in range(length) if 0 <= i + by < length]
    return lax.ppermute(value, axis, pairs)


def build_band(tile_set, col_ids, live_count, first_block):
    block_count = tile_set.shape[0]
    row_ids = first_block + jnp.arange(block_count, dtype=jnp.int32)
    offset = col_ids - row_ids[:, None] + HB
    live_mask = jnp.arange(TPB, dtype=jnp.int32)[None, :] < live_count[:, None]
    tiles = tile_set.astype(jnp.float32)
    bands = []
    for o in range(2 * HB + 1):
        pick = ((offset == o) & live_mask).astype(jnp.float32)
        bands.append(jnp.sum(pick[:, :, None, None] * tiles, axis=1).astype(jnp.bfloat16))
    return bands


def band_product(bands, extended):
    block_count = bands[0].shape[0]
    total = None
    for offset in range(2 * HB + 1):
        term = jnp.einsum(
            "bpq,bqf->bpf",
            bands[offset],
            extended[offset : offset + block_count],
            preferred_element_type=jnp.float32,
        )
        total = term if total is None else total + term
    return total


def pair_weight(conv_weight):
    taps, chan_in, width = conv_weight.shape
    eye = jnp.eye(2, dtype=conv_weight.dtype)
    blocks = [jnp.kron(eye, conv_weight[k]) for k in range(taps)]
    rows_in = jnp.arange(2 * chan_in, dtype=jnp.int32)[:, None]
    cols_out = jnp.arange(2 * width, dtype=jnp.int32)[None, :]
    place = (cols_out == rows_in // chan_in * width + rows_in % chan_in).astype(conv_weight.dtype)
    return jnp.concatenate(blocks + [place], axis=0)


def block_diag(weight, steps):
    return jnp.kron(jnp.eye(steps, dtype=weight.dtype), weight)


def stage(
    inputs, conv_weight, conv_bias, tile_values, tile_cols, tile_count, cheb_weight, cheb_bias
):
    row_count, flat_width = inputs.shape
    chan_in = conv_weight.shape[1]
    chan_out = cheb_weight.shape[2]
    steps_dev = flat_width // chan_in
    block_count, block_rows = (tile_values.shape[0], tile_values.shape[2])
    feat_width = steps_dev * chan_out
    earlier = passed_along(inputs, "tm", 1)
    wpair = pair_weight(conv_weight)
    pair_w = 2 * chan_in
    pieces = []
    for p in range(steps_dev // 2):
        w_new, w_mid, w_old, w_place = (wpair[i * pair_w : (i + 1) * pair_w] for i in range(4))
        newest = inputs[:, p * pair_w : (p + 1) * pair_w]
        cur_l = [newest, newest]
        cur_w = [w_new, w_place]
        prev_l = []
        prev_w = []
        for lag, w in ((1, w_mid), (2, w_old)):
            q = p - lag
            if q >= 0:
                cur_l.append(inputs[:, q * pair_w : (q + 1) * pair_w])
                cur_w.append(w)
            else:
                q += steps_dev // 2
                prev_l.append(earlier[:, q * pair_w : (q + 1) * pair_w])
                prev_w.append(w)
        mixed = jnp.dot(
            jnp.concatenate(cur_l, axis=1), jnp.concatenate(cur_w, axis=0), preferred_element_type=jnp.float32
        )
        mixed = mixed + jnp.dot(
            jnp.concatenate(prev_l, axis=1), jnp.concatenate(prev_w, axis=0), preferred_element_type=jnp.float32
        )
        for tt in range(2):
            lo = tt * 2 * chan_out
            linear = mixed[:, lo : lo + chan_out] + conv_bias[:chan_out]
            gate = mixed[:, lo + chan_out : lo + 2 * chan_out] + conv_bias[chan_out:]
            pieces.append(linear * jax.nn.sigmoid(gate))
    flat_features = jnp.concatenate(pieces, axis=1).astype(jnp.bfloat16)
    first_block = lax.axis_index("node") * block_count
    band_tiles = build_band(tile_values, tile_cols, tile_count, first_block)
    node_count = lax.axis_size("node")
    to_right = [(i, i + 1) for i in range(node_count - 1)]
    to_left = [(i + 1, i) for i in range(node_count - 1)]
    rim = HB * block_rows
    edge_ids = list(range(HB)) + list(range(block_count - HB, block_count))
    halo_band = []
    for b in edge_ids:
        terms = []
        for o in range(2 * HB + 1):
            j = b + o
            if j < HB or j >= block_count + HB:
                terms.append(band_tiles[o][b])
        while len(terms) < HB:
            terms.append(jnp.zeros_like(band_tiles[0][0]))
        halo_band.append(jnp.stack(terms))
    halo_band = jnp.stack(halo_band)

    def halo_blocks(left, right):
        lb = left.reshape(HB, block_rows, feat_width)
        rb = right.reshape(HB, block_rows, feat_width)
        picks = []
        for b in edge_ids:
            terms = []
            for o in range(2 * HB + 1):
                j = b + o
                if j < HB:
                    terms.append(lb[j])
                elif j >= block_count + HB:
                    terms.append(rb[j - block_count - HB])
            while len(terms) < HB:
                terms.append(terms[-1])
            picks.append(jnp.stack(terms))
        return jnp.stack(picks)

    def halo_part(left, right):
        part = jnp.einsum(
            "bkpq,bkqf->bpf", halo_band, halo_blocks(left, right), preferred_element_type=jnp.float32
        )
        middle = jnp.zeros((block_count - 2 * HB, block_rows, feat_width), jnp.float32)
        return jnp.concatenate([part[:HB], middle, part[HB:]], axis=0)

    def own_part(values):
        padded = jnp.pad(values.reshape(block_count, block_rows, feat_width), ((HB, HB), (0, 0), (0, 0)))
        return band_product(band_tiles, padded)

    feat_left = lax.ppermute(flat_features[row_count - rim :], "node", to_right)
    feat_right = lax.ppermute(flat_features[:rim], "node", to_left)
    one_own = own_part(flat_features)
    order_one = (one_own + halo_part(feat_left, feat_right)).astype(jnp.bfloat16)
    order_one = order_one.reshape(row_count, feat_width)
    one_left = lax.ppermute(order_one[row_count - rim :], "node", to_right)
    one_right = lax.ppermute(order_one[:rim], "node", to_left)
    two_own = own_part(order_one)
    kron = [block_diag(cheb_weight[k], steps_dev) for k in range(3)]
    early = jnp.dot(
        jnp.concatenate([flat_features, order_one], axis=1),
        jnp.concatenate(kron[:2], axis=0),
        preferred_element_type=jnp.float32,
    ) + jnp.tile(cheb_bias, steps_dev)
    order_two = (two_own + halo_part(one_left, one_right)).reshape(row_count, feat_width)
    cheb_two = (2.0 * order_two - flat_features.astype(jnp.float32)).astype(jnp.bfloat16)
    result = early + jnp.dot(cheb_two, kron[2], preferred_element_type=jnp.float32)
    return jax.nn.relu(result).astype(jnp.bfloat16).reshape(row_count, steps_dev, chan_out)


def solution(mesh):
    placed = (
        P("node", "tm"),
        P(),
        P(),
        P("node", None, None, None),
        P("node", None),
        P("node"),
        P(),
        P(),
    )
    return jax.shard_map(stage, mesh=mesh, in_specs=placed, out_specs=P("node", "tm", None), check_vma=False)
```

```python
import jax
import jax.numpy as jnp
from jax import lax
from jax.sharding import PartitionSpec as P

HB = 2
TPB = 4


def passed_along(value, axis, by):
    length = lax.axis_size(axis)
    pairs = [(i, i + by) for i in range(length) if 0 <= i + by < length]
    return lax.ppermute(value, axis, pairs)


def build_band(tile_set, col_ids, live_count, first_block):
    block_count = tile_set.shape[0]
    row_ids = first_block + jnp.arange(block_count, dtype=jnp.int32)
    offset = col_ids - row_ids[:, None] + HB
    live_mask = jnp.arange(TPB, dtype=jnp.int32)[None, :] < live_count[:, None]
    tiles = tile_set.astype(jnp.float32)
    bands = []
    for o in range(2 * HB + 1):
        pick = ((offset == o) & live_mask).astype(jnp.float32)
        bands.append(jnp.sum(pick[:, :, None, None] * tiles, axis=1).astype(jnp.bfloat16))
    return bands


def band_product(bands, extended):
    block_count = bands[0].shape[0]
    total = None
    for offset in range(2 * HB + 1):
        term = jnp.einsum(
            "bpq,bqf->bpf",
            bands[offset],
            extended[offset : offset + block_count],
            preferred_element_type=jnp.float32,
        )
        total = term if total is None else total + term
    return total


def pair_weight(conv_weight):
    taps, chan_in, width = conv_weight.shape
    eye = jnp.eye(2, dtype=conv_weight.dtype)
    blocks = [jnp.kron(eye, conv_weight[k]) for k in range(taps)]
    rows_in = jnp.arange(2 * chan_in, dtype=jnp.int32)[:, None]
    cols_out = jnp.arange(2 * width, dtype=jnp.int32)[None, :]
    place = (cols_out == rows_in // chan_in * width + rows_in % chan_in).astype(conv_weight.dtype)
    return jnp.concatenate(blocks + [place], axis=0)


def block_diag(weight, steps):
    return jnp.kron(jnp.eye(steps, dtype=weight.dtype), weight)


def stage(
    inputs, conv_weight, conv_bias, tile_values, tile_cols, tile_count, cheb_weight, cheb_bias
):
    row_count, flat_width = inputs.shape
    chan_in = conv_weight.shape[1]
    chan_out = cheb_weight.shape[2]
    steps_dev = flat_width // chan_in
    block_count, block_rows = (tile_values.shape[0], tile_values.shape[2])
    feat_width = steps_dev * chan_out
    earlier = passed_along(inputs, "tm", 1)
    wpair = pair_weight(conv_weight)
    bias_row = jnp.tile(conv_bias, 2)[None, :]
    pair_w = 2 * chan_in
    pieces = []
    for p in range(steps_dev // 2):
        w_new, w_mid, w_old, w_place = (wpair[i * pair_w : (i + 1) * pair_w] for i in range(4))
        newest = inputs[:, p * pair_w : (p + 1) * pair_w]
        cur_l = [newest, newest]
        cur_w = [w_new, w_place]
        prev_l = []
        prev_w = []
        for lag, w in ((1, w_mid), (2, w_old)):
            q = p - lag
            if q >= 0:
                cur_l.append(inputs[:, q * pair_w : (q + 1) * pair_w])
                cur_w.append(w)
            else:
                q += steps_dev // 2
                prev_l.append(earlier[:, q * pair_w : (q + 1) * pair_w])
                prev_w.append(w)
        mixed = jnp.dot(
            jnp.concatenate(cur_l, axis=1), jnp.concatenate(cur_w, axis=0), preferred_element_type=jnp.float32
        )
        mixed = mixed + jnp.dot(
            jnp.concatenate(prev_l, axis=1), jnp.concatenate(prev_w, axis=0), preferred_element_type=jnp.float32
        )
        mixed = mixed + bias_row
        for tt in range(2):
            lo = tt * 2 * chan_out
            linear = mixed[:, lo : lo + chan_out]
            gate = mixed[:, lo + chan_out : lo + 2 * chan_out]
            pieces.append(linear * jax.nn.sigmoid(gate))
    flat_features = jnp.concatenate(pieces, axis=1).astype(jnp.bfloat16)
    first_block = lax.axis_index("node") * block_count
    band_tiles = build_band(tile_values, tile_cols, tile_count, first_block)
    node_count = lax.axis_size("node")
    to_right = [(i, i + 1) for i in range(node_count - 1)]
    to_left = [(i + 1, i) for i in range(node_count - 1)]
    rim = HB * block_rows
    edge_ids = list(range(HB)) + list(range(block_count - HB, block_count))
    halo_band = []
    for b in edge_ids:
        terms = []
        for o in range(2 * HB + 1):
            j = b + o
            if j < HB or j >= block_count + HB:
                terms.append(band_tiles[o][b])
        while len(terms) < HB:
            terms.append(jnp.zeros_like(band_tiles[0][0]))
        halo_band.append(jnp.stack(terms))
    halo_band = jnp.stack(halo_band)

    def halo_blocks(left, right):
        lb = left.reshape(HB, block_rows, feat_width)
        rb = right.reshape(HB, block_rows, feat_width)
        picks = []
        for b in edge_ids:
            terms = []
            for o in range(2 * HB + 1):
                j = b + o
                if j < HB:
                    terms.append(lb[j])
                elif j >= block_count + HB:
                    terms.append(rb[j - block_count - HB])
            while len(terms) < HB:
                terms.append(terms[-1])
            picks.append(jnp.stack(terms))
        return jnp.stack(picks)

    def halo_part(left, right):
        part = jnp.einsum(
            "bkpq,bkqf->bpf", halo_band, halo_blocks(left, right), preferred_element_type=jnp.float32
        )
        middle = jnp.zeros((block_count - 2 * HB, block_rows, feat_width), jnp.float32)
        return jnp.concatenate([part[:HB], middle, part[HB:]], axis=0)

    def own_part(values):
        padded = jnp.pad(values.reshape(block_count, block_rows, feat_width), ((HB, HB), (0, 0), (0, 0)))
        return band_product(band_tiles, padded)

    feat_left = lax.ppermute(flat_features[row_count - rim :], "node", to_right)
    feat_right = lax.ppermute(flat_features[:rim], "node", to_left)
    one_own = own_part(flat_features)
    order_one = (one_own + halo_part(feat_left, feat_right)).astype(jnp.bfloat16)
    order_one = order_one.reshape(row_count, feat_width)
    one_left = lax.ppermute(order_one[row_count - rim :], "node", to_right)
    one_right = lax.ppermute(order_one[:rim], "node", to_left)
    two_own = own_part(order_one)
    kron = [block_diag(cheb_weight[k], steps_dev) for k in range(3)]
    early = jnp.dot(
        jnp.concatenate([flat_features, order_one], axis=1),
        jnp.concatenate(kron[:2], axis=0),
        preferred_element_type=jnp.float32,
    ) + jnp.tile(cheb_bias, steps_dev)
    order_two = (two_own + halo_part(one_left, one_right)).reshape(row_count, feat_width)
    cheb_two = (2.0 * order_two - flat_features.astype(jnp.float32)).astype(jnp.bfloat16)
    result = early + jnp.dot(cheb_two, kron[2], preferred_element_type=jnp.float32)
    return jax.nn.relu(result).astype(jnp.bfloat16).reshape(row_count, steps_dev, chan_out)


def solution(mesh):
    placed = (
        P("node", "tm"),
        P(),
        P(),
        P("node", None, None, None),
        P("node", None),
        P("node"),
        P(),
        P(),
    )
    return jax.shard_map(stage, mesh=mesh, in_specs=placed, out_specs=P("node", "tm", None), check_vma=False)
```

```python
import jax
import jax.numpy as jnp
from jax import lax
from jax.sharding import PartitionSpec as P

HB = 2
TPB = 4


def passed_along(value, axis, by):
    length = lax.axis_size(axis)
    pairs = [(i, i + by) for i in range(length) if 0 <= i + by < length]
    return lax.ppermute(value, axis, pairs)


def build_band(tile_set, col_ids, live_count, first_block):
    block_count = tile_set.shape[0]
    row_ids = first_block + jnp.arange(block_count, dtype=jnp.int32)
    offset = col_ids - row_ids[:, None] + HB
    live_mask = jnp.arange(TPB, dtype=jnp.int32)[None, :] < live_count[:, None]
    tiles = tile_set.astype(jnp.float32)
    bands = []
    for o in range(2 * HB + 1):
        pick = ((offset == o) & live_mask).astype(jnp.float32)
        bands.append(jnp.sum(pick[:, :, None, None] * tiles, axis=1).astype(jnp.bfloat16))
    return bands


def band_product(bands, extended):
    block_count = bands[0].shape[0]
    total = None
    for offset in range(2 * HB + 1):
        term = jnp.einsum(
            "bpq,bqf->bpf",
            bands[offset],
            extended[offset : offset + block_count],
            preferred_element_type=jnp.float32,
        )
        total = term if total is None else total + term
    return total


def block_diag(weight, steps):
    return jnp.kron(jnp.eye(steps, dtype=weight.dtype), weight)


def stage(
    inputs, conv_weight, conv_bias, tile_values, tile_cols, tile_count, cheb_weight, cheb_bias
):
    row_count, flat_width = inputs.shape
    chan_in = conv_weight.shape[1]
    chan_out = cheb_weight.shape[2]
    steps_dev = flat_width // chan_in
    block_count, block_rows = (tile_values.shape[0], tile_values.shape[2])
    feat_width = steps_dev * chan_out
    earlier = passed_along(inputs, "tm", 1)
    taps = conv_weight.shape[0]
    s_idx = jnp.arange(steps_dev, dtype=jnp.int32)[:, None]
    t_idx = jnp.arange(steps_dev, dtype=jnp.int32)[None, :]
    w_cur = 0.0
    w_prev = 0.0
    for k in range(taps):
        shift_cur = (s_idx == t_idx - 2 * k).astype(jnp.float32)
        shift_prev = (s_idx - steps_dev == t_idx - 2 * k).astype(jnp.float32)
        tap = conv_weight[k].astype(jnp.float32)
        w_cur = w_cur + jnp.kron(shift_cur, tap)
        w_prev = w_prev + jnp.kron(shift_prev, tap)
    w_cur = w_cur.astype(jnp.bfloat16)
    w_prev = w_prev.astype(jnp.bfloat16)
    rows_in = jnp.arange(steps_dev * chan_in, dtype=jnp.int32)[:, None]
    cols_out = jnp.arange(steps_dev * 2 * chan_out, dtype=jnp.int32)[None, :]
    place = (cols_out == rows_in // chan_in * (2 * chan_out) + rows_in % chan_in).astype(jnp.bfloat16)
    mixed = jnp.dot(inputs, w_cur, preferred_element_type=jnp.float32)
    mixed = mixed + jnp.dot(inputs, place, preferred_element_type=jnp.float32)
    mixed = mixed + jnp.dot(earlier, w_prev, preferred_element_type=jnp.float32)
    mixed = mixed + jnp.tile(conv_bias, steps_dev)[None, :]
    pieces = []
    for t in range(steps_dev):
        lo = t * 2 * chan_out
        linear = mixed[:, lo : lo + chan_out]
        gate = mixed[:, lo + chan_out : lo + 2 * chan_out]
        pieces.append(linear * jax.nn.sigmoid(gate))
    flat_features = jnp.concatenate(pieces, axis=1).astype(jnp.bfloat16)
    first_block = lax.axis_index("node") * block_count
    band_tiles = build_band(tile_values, tile_cols, tile_count, first_block)
    node_count = lax.axis_size("node")
    to_right = [(i, i + 1) for i in range(node_count - 1)]
    to_left = [(i + 1, i) for i in range(node_count - 1)]
    rim = HB * block_rows
    edge_ids = list(range(HB)) + list(range(block_count - HB, block_count))
    halo_band = []
    for b in edge_ids:
        terms = []
        for o in range(2 * HB + 1):
            j = b + o
            if j < HB or j >= block_count + HB:
                terms.append(band_tiles[o][b])
        while len(terms) < HB:
            terms.append(jnp.zeros_like(band_tiles[0][0]))
        halo_band.append(jnp.stack(terms))
    halo_band = jnp.stack(halo_band)

    def halo_blocks(left, right):
        lb = left.reshape(HB, block_rows, feat_width)
        rb = right.reshape(HB, block_rows, feat_width)
        picks = []
        for b in edge_ids:
            terms = []
            for o in range(2 * HB + 1):
                j = b + o
                if j < HB:
                    terms.append(lb[j])
                elif j >= block_count + HB:
                    terms.append(rb[j - block_count - HB])
            while len(terms) < HB:
                terms.append(terms[-1])
            picks.append(jnp.stack(terms))
        return jnp.stack(picks)

    def halo_part(left, right):
        part = jnp.einsum(
            "bkpq,bkqf->bpf", halo_band, halo_blocks(left, right), preferred_element_type=jnp.float32
        )
        middle = jnp.zeros((block_count - 2 * HB, block_rows, feat_width), jnp.float32)
        return jnp.concatenate([part[:HB], middle, part[HB:]], axis=0)

    def own_part(values):
        padded = jnp.pad(values.reshape(block_count, block_rows, feat_width), ((HB, HB), (0, 0), (0, 0)))
        return band_product(band_tiles, padded)

    feat_left = lax.ppermute(flat_features[row_count - rim :], "node", to_right)
    feat_right = lax.ppermute(flat_features[:rim], "node", to_left)
    one_own = own_part(flat_features)
    order_one = (one_own + halo_part(feat_left, feat_right)).astype(jnp.bfloat16)
    order_one = order_one.reshape(row_count, feat_width)
    one_left = lax.ppermute(order_one[row_count - rim :], "node", to_right)
    one_right = lax.ppermute(order_one[:rim], "node", to_left)
    two_own = own_part(order_one)
    kron = [block_diag(cheb_weight[k], steps_dev) for k in range(3)]
    early = jnp.dot(
        jnp.concatenate([flat_features, order_one], axis=1),
        jnp.concatenate(kron[:2], axis=0),
        preferred_element_type=jnp.float32,
    ) + jnp.tile(cheb_bias, steps_dev)
    order_two = (two_own + halo_part(one_left, one_right)).reshape(row_count, feat_width)
    cheb_two = (2.0 * order_two - flat_features.astype(jnp.float32)).astype(jnp.bfloat16)
    result = early + jnp.dot(cheb_two, kron[2], preferred_element_type=jnp.float32)
    return jax.nn.relu(result).astype(jnp.bfloat16).reshape(row_count, steps_dev, chan_out)


def solution(mesh):
    placed = (
        P("node", "tm"),
        P(),
        P(),
        P("node", None, None, None),
        P("node", None),
        P("node"),
        P(),
        P(),
    )
    return jax.shard_map(
        stage, mesh=mesh, in_specs=placed, out_specs=P("node", "tm", None), check_vma=False
    )
```

```python
import jax
import jax.numpy as jnp
from jax import lax
from jax.sharding import PartitionSpec as P

HB = 2
TPB = 4


def passed_along(value, axis, by):
    length = lax.axis_size(axis)
    pairs = [(i, i + by) for i in range(length) if 0 <= i + by < length]
    return lax.ppermute(value, axis, pairs)


def build_band(tile_set, col_ids, live_count, first_block):
    block_count = tile_set.shape[0]
    row_ids = first_block + jnp.arange(block_count, dtype=jnp.int32)
    offset = col_ids - row_ids[:, None] + HB
    live_mask = jnp.arange(TPB, dtype=jnp.int32)[None, :] < live_count[:, None]
    tiles = tile_set.astype(jnp.float32)
    bands = []
    for o in range(2 * HB + 1):
        pick = ((offset == o) & live_mask).astype(jnp.float32)
        bands.append(jnp.sum(pick[:, :, None, None] * tiles, axis=1).astype(jnp.bfloat16))
    return bands


def band_product(bands, extended):
    block_count = bands[0].shape[0]
    total = None
    for offset in range(2 * HB + 1):
        term = jnp.einsum(
            "bpq,bqf->bpf",
            bands[offset],
            extended[offset : offset + block_count],
            preferred_element_type=jnp.float32,
        )
        total = term if total is None else total + term
    return total


def pair_weight(conv_weight):
    taps, chan_in, width = conv_weight.shape
    eye = jnp.eye(2, dtype=conv_weight.dtype)
    blocks = [jnp.kron(eye, conv_weight[k]) for k in range(taps)]
    rows_in = jnp.arange(2 * chan_in, dtype=jnp.int32)[:, None]
    cols_out = jnp.arange(2 * width, dtype=jnp.int32)[None, :]
    place = (cols_out == rows_in // chan_in * width + rows_in % chan_in).astype(conv_weight.dtype)
    return jnp.concatenate(blocks + [place], axis=0)


def block_diag(weight, steps):
    return jnp.kron(jnp.eye(steps, dtype=weight.dtype), weight)


def stage(
    inputs, conv_weight, conv_bias, tile_values, tile_cols, tile_count, cheb_weight, cheb_bias
):
    row_count, flat_width = inputs.shape
    chan_in = conv_weight.shape[1]
    chan_out = cheb_weight.shape[2]
    steps_dev = flat_width // chan_in
    block_count, block_rows = (tile_values.shape[0], tile_values.shape[2])
    feat_width = steps_dev * chan_out
    earlier = passed_along(inputs, "tm", 1)
    wpair = pair_weight(conv_weight)
    bias_row = jnp.tile(conv_bias, 2)[None, :]
    pair_w = 2 * chan_in
    pieces = []
    for p in range(steps_dev // 2):
        w_new, w_mid, w_old, w_place = (wpair[i * pair_w : (i + 1) * pair_w] for i in range(4))
        newest = inputs[:, p * pair_w : (p + 1) * pair_w]
        cur_l = [newest, newest]
        cur_w = [w_new, w_place]
        prev_l = []
        prev_w = []
        for lag, w in ((1, w_mid), (2, w_old)):
            q = p - lag
            if q >= 0:
                cur_l.append(inputs[:, q * pair_w : (q + 1) * pair_w])
                cur_w.append(w)
            else:
                q += steps_dev // 2
                prev_l.append(earlier[:, q * pair_w : (q + 1) * pair_w])
                prev_w.append(w)
        mixed = jnp.dot(
            jnp.concatenate(cur_l, axis=1), jnp.concatenate(cur_w, axis=0), preferred_element_type=jnp.float32
        )
        mixed = mixed + jnp.dot(
            jnp.concatenate(prev_l, axis=1), jnp.concatenate(prev_w, axis=0), preferred_element_type=jnp.float32
        )
        mixed = mixed + bias_row
        for tt in range(2):
            lo = tt * 2 * chan_out
            linear = mixed[:, lo : lo + chan_out]
            gate = mixed[:, lo + chan_out : lo + 2 * chan_out]
            pieces.append(linear * jax.nn.sigmoid(gate))
    flat_features = jnp.concatenate(pieces, axis=1).astype(jnp.bfloat16)
    first_block = lax.axis_index("node") * block_count
    band_tiles = build_band(tile_values, tile_cols, tile_count, first_block)
    node_count = lax.axis_size("node")
    to_right = [(i, i + 1) for i in range(node_count - 1)]
    to_left = [(i + 1, i) for i in range(node_count - 1)]
    rim = HB * block_rows
    edge_ids = list(range(HB)) + list(range(block_count - HB, block_count))
    halo_band = []
    for b in edge_ids:
        terms = []
        for o in range(2 * HB + 1):
            j = b + o
            if j < HB or j >= block_count + HB:
                terms.append(band_tiles[o][b])
        while len(terms) < HB:
            terms.append(jnp.zeros_like(band_tiles[0][0]))
        halo_band.append(jnp.stack(terms))
    halo_band = jnp.stack(halo_band)

    def halo_blocks(left, right):
        lb = left.reshape(HB, block_rows, feat_width)
        rb = right.reshape(HB, block_rows, feat_width)
        picks = []
        for b in edge_ids:
            terms = []
            for o in range(2 * HB + 1):
                j = b + o
                if j < HB:
                    terms.append(lb[j])
                elif j >= block_count + HB:
                    terms.append(rb[j - block_count - HB])
            while len(terms) < HB:
                terms.append(terms[-1])
            picks.append(jnp.stack(terms))
        return jnp.stack(picks)

    def halo_part(left, right):
        part = jnp.einsum(
            "bkpq,bkqf->bpf", halo_band, halo_blocks(left, right), preferred_element_type=jnp.float32
        )
        middle = jnp.zeros((block_count - 2 * HB, block_rows, feat_width), jnp.float32)
        return jnp.concatenate([part[:HB], middle, part[HB:]], axis=0)

    def own_part(values):
        padded = jnp.pad(values.reshape(block_count, block_rows, feat_width), ((HB, HB), (0, 0), (0, 0)))
        return band_product(band_tiles, padded)

    feat_left = lax.ppermute(flat_features[row_count - rim :], "node", to_right)
    feat_right = lax.ppermute(flat_features[:rim], "node", to_left)
    one_own = own_part(flat_features)
    order_one = (one_own + halo_part(feat_left, feat_right)).astype(jnp.bfloat16)
    order_one = order_one.reshape(row_count, feat_width)
    one_left = lax.ppermute(order_one[row_count - rim :], "node", to_right)
    one_right = lax.ppermute(order_one[:rim], "node", to_left)
    two_own = own_part(order_one)
    late_weight, _ = lax.optimization_barrier((cheb_weight, one_own))
    kron = [block_diag(late_weight[k], steps_dev) for k in range(3)]
    early = jnp.dot(
        jnp.concatenate([flat_features, order_one], axis=1),
        jnp.concatenate(kron[:2], axis=0),
        preferred_element_type=jnp.float32,
    ) + jnp.tile(cheb_bias, steps_dev)
    order_two = (two_own + halo_part(one_left, one_right)).reshape(row_count, feat_width)
    cheb_two = (2.0 * order_two - flat_features.astype(jnp.float32)).astype(jnp.bfloat16)
    result = early + jnp.dot(cheb_two, kron[2], preferred_element_type=jnp.float32)
    return jax.nn.relu(result).astype(jnp.bfloat16).reshape(row_count, steps_dev, chan_out)


def solution(mesh):
    placed = (
        P("node", "tm"),
        P(),
        P(),
        P("node", None, None, None),
        P("node", None),
        P("node"),
        P(),
        P(),
    )
    return jax.shard_map(
        stage, mesh=mesh, in_specs=placed, out_specs=P("node", "tm", None), check_vma=False
    )
```
